256 devices in a mesh: stream: 8 (over y, core), seq: 32 (over x, z).
Axes of the slice: x: 4, y: 4, z: 8, core: 2. Of those that a mesh axis runs over, the one named last changes fastest.
Arguments:
- inner_x: bfloat16 [32768, 4096], P(('stream', 'seq')), parts along dimension 0, may hold values from -6 to 6
- inner_gate: bfloat16 [32768, 4096], P(('stream', 'seq')), parts along dimension 0, may hold values from -6 to 6
- conv_weight: float32 [4, 4096], replicated, may hold values from -3 to 3
- conv_bias: float32 [4096], replicated, may hold values from -3 to 3
- step_low: bfloat16 [32768, 256], P(('stream', 'seq')), parts along dimension 0, may hold values from -5 to 48
- step_proj: bfloat16 [256, 4096], replicated, may hold values from -1 to 2
- step_bias: float32 [4096], replicated, may hold values from -4.5 to -3.5
- decay_log: float32 [16, 4096], replicated, may hold values from -12 to 2
- state_in: float32 [32768, 16], P(('stream', 'seq')), parts along dimension 0, may hold values from -8 to 8
- state_out: float32 [32768, 16], P(('stream', 'seq')), parts along dimension 0, may hold values from -1.5 to 1.5
- skip_gain: float32 [4096], replicated, may hold values from 0.5 to 1.5
- query_heads: bfloat16 [32768, 4096], P(('stream', 'seq')), parts along dimension 0, may hold values from -6 to 6
- key_heads: bfloat16 [32768, 1024], P(('stream', 'seq')), parts along dimension 0, may hold values from -6 to 6
- value_heads: bfloat16 [32768, 1024], P(('stream', 'seq')), parts along dimension 0, may hold values from -6 to 6
Outputs:
- mamba_out: bfloat16 [32768, 4096], P(('stream', 'seq')), parts along dimension 0
- attention_out: bfloat16 [32768, 4096], P(('stream', 'seq')), parts along dimension 0
The draws below stay inside these ranges and needn't reach their ends.
There are 8 independent parts, one for each index of `stream`. The reference program is written for one: setup_inputs(seed, part) draws one part's arguments, and reference() takes and returns one part's arrays. A program takes and returns all parts, laid end to end along the dimension named above; an argument that names none is the same for every part. Nothing has to cross between parts.
All inputs are finite; a program needn't handle non-finite values.
Results may differ from the reference program's by a relative error of at most 0.007.
Values may be sent and summed in bfloat16 or wider, within the bound.
No kernel may reach another device: no remote copies, remote signals or barrier semaphores. Data moves between devices by JAX's collectives and lax.ppermute only.
A program may use at most 128 MiB of HBM per device.

```python
import math
import jax
import jax.numpy as jnp
from jax import lax

INNER_DIM = 4096
STATE_ENTRIES = 16
CONV_WIDTH = 4
DT_RANK = 256
QHEADS = 32
KVHEADS = 8
HEAD_DIM = 128
SEQ_LEN = 4096


def document_mask(key):
    places = jax.random.randint(jax.random.fold_in(key, 5), (3,), 0, SEQ_LEN)
    return jnp.any(jnp.arange(SEQ_LEN)[:, None] == places[None, :], axis=1)


def draw_step_low(key, part):
    base_offset = jnp.clip(jax.random.normal(jax.random.fold_in(key, 21), (SEQ_LEN, DT_RANK), jnp.float32), -4.0, 4.0)
    first_entry = 0.3 * jnp.clip(jax.random.normal(jax.random.fold_in(key, 22), (SEQ_LEN,), jnp.float32), -4.0, 4.0)
    target = 0.0093 * SEQ_LEN
    lifted_values = target + 4.0
    first_entry = first_entry + jnp.where(document_mask(key), lifted_values, 0.0)
    return base_offset.at[:, 0].set(first_entry).astype(jnp.bfloat16)


def draw_step_proj(key, part):
    rest = jnp.clip(jax.random.normal(jax.random.fold_in(key, 23), (DT_RANK, INNER_DIM), jnp.float32), -4.0, 4.0) / math.sqrt(DT_RANK)
    first_entry = jax.random.uniform(jax.random.fold_in(key, 24), (INNER_DIM,), jnp.float32, 0.8, 1.2)
    return rest.at[0].set(first_entry).astype(jnp.bfloat16)


def draw_decay_log(key, part):
    share = 0.5
    slow = jax.random.uniform(jax.random.fold_in(key, 41), (INNER_DIM,), jnp.float32) < share
    low = jax.random.uniform(jax.random.fold_in(key, 42), (INNER_DIM,), jnp.float32, math.log(0.5 / SEQ_LEN), math.log(1.5 / SEQ_LEN))
    high = jax.random.uniform(jax.random.fold_in(key, 43), (INNER_DIM,), jnp.float32, math.log(1.0 / 50.0), math.log(1.0 / 20.0))
    rates = jnp.where(slow, low, high)
    factor = jnp.log(0.5 + jnp.arange(STATE_ENTRIES, dtype=jnp.float32) / STATE_ENTRIES)
    return (rates[None, :] + factor[:, None] - math.log(0.03)).astype(jnp.float32)


def draw_state_in(key, part):
    base_offset = jnp.clip(jax.random.normal(jax.random.fold_in(key, 51), (SEQ_LEN, STATE_ENTRIES), jnp.float32), -4.0, 4.0)
    base_offset = base_offset * jnp.where(document_mask(key), 0.03, 1.0)[:, None]
    return base_offset.astype(jnp.float32)


def paired(key):
    queries = jnp.clip(jax.random.normal(jax.random.fold_in(key, 31), (SEQ_LEN, QHEADS, HEAD_DIM), jnp.float32), -4.0, 4.0)
    keys = jnp.clip(jax.random.normal(jax.random.fold_in(key, 32), (SEQ_LEN, KVHEADS, HEAD_DIM), jnp.float32), -4.0, 4.0)
    return (queries.reshape(SEQ_LEN, QHEADS * HEAD_DIM), keys.reshape(SEQ_LEN, KVHEADS * HEAD_DIM))


def draw_query_heads(key, part):
    return paired(key)[0].astype(jnp.bfloat16)


def draw_key_heads(key, part):
    return paired(key)[1].astype(jnp.bfloat16)


def block_scale(own_key, shape, pieces, smallest, high):
    level = 1.0
    for axis_at, blocks in pieces:
        heights = jax.random.uniform(jax.random.fold_in(jax.random.fold_in(own_key, 6), axis_at), (blocks,), jnp.float32, smallest / len(pieces), high / len(pieces))
        level = level * jnp.repeat(jnp.exp(heights), shape[axis_at] // blocks).reshape((-1,) + (1,) * (len(shape) - 1 - axis_at))
    return level


def bell_draw(rng, dims, scale, most, shards=(), held_as=jnp.bfloat16):
    entries = jax.random.normal(rng, dims, jnp.float32) * scale
    if len(shards) > 0:
        entries = block_scale(rng, dims, shards, -0.22, 0.18) * entries
    return jnp.clip(entries, min=-most, max=most).astype(held_as)


def setup_inputs(seed: int = 0, part: int = 0) -> dict:
    seeds = jax.random.split(jax.random.key(seed), 15)
    part_keys = jax.random.split(jax.random.fold_in(seeds[14], part), 15)
    return {
        "inner_x": bell_draw(part_keys[0], (SEQ_LEN, INNER_DIM), 1.0, 6.0, ((0, 32),)),
        "inner_gate": bell_draw(part_keys[1], (SEQ_LEN, INNER_DIM), 1.0, 6.0, ((0, 32),)),
        "conv_weight": bell_draw(seeds[2], (CONV_WIDTH, INNER_DIM), CONV_WIDTH ** -0.5, 3.0, (), jnp.float32),
        "conv_bias": bell_draw(seeds[3], (INNER_DIM,), 0.5, 3.0, (), jnp.float32),
        "step_low": draw_step_low(jax.random.fold_in(jax.random.fold_in(seeds[14], part), 71), part),
        "step_proj": draw_step_proj(jax.random.fold_in(seeds[14], 71), part),
        "step_bias": jnp.clip(jax.random.uniform(seeds[6], (INNER_DIM,), jnp.float32, -4.5, -3.5), -4.5, -3.5),
        "decay_log": draw_decay_log(jax.random.fold_in(seeds[14], 71), part),
        "state_in": draw_state_in(jax.random.fold_in(jax.random.fold_in(seeds[14], part), 71), part),
        "state_out": bell_draw(part_keys[9], (SEQ_LEN, STATE_ENTRIES), 0.25, 1.5, ((0, 32),), jnp.float32),
        "skip_gain": jnp.clip(jax.random.uniform(seeds[10], (INNER_DIM,), jnp.float32, 0.5, 1.5), 0.5, 1.5),
        "query_heads": draw_query_heads(jax.random.fold_in(jax.random.fold_in(seeds[14], part), 71), part),
        "key_heads": draw_key_heads(jax.random.fold_in(jax.random.fold_in(seeds[14], part), 71), part),
        "value_heads": bell_draw(part_keys[13], (SEQ_LEN, KVHEADS * HEAD_DIM), 1.0, 6.0, ((0, 32),)),
    }


def convolve(padded, conv_weight, conv_bias):
    reach = conv_weight.shape[0] - 1
    length = padded.shape[0] - reach
    total = jnp.zeros((length, padded.shape[1]), jnp.float32)
    for index in range(reach + 1):
        total = total + conv_weight[index][None, :] * padded[index:index + length].astype(jnp.float32)
    return jax.nn.silu(total + conv_bias[None, :])


def reference(inner_x, inner_gate, conv_weight, conv_bias, step_low, step_proj, step_bias, decay_log, state_in, state_out, skip_gain, query_heads, key_heads, value_heads):
    reach = conv_weight.shape[0] - 1
    padded = jnp.concatenate([jnp.zeros((reach, inner_x.shape[1]), inner_x.dtype), inner_x], 0)
    conv = convolve(padded, conv_weight, conv_bias)
    step = jax.nn.softplus(jnp.dot(step_low, step_proj, preferred_element_type=jnp.float32) + step_bias[None, :])
    rate = -jnp.exp(decay_log)

    def advance(state, row):
        step_row, conv_row, in_row, out_row = row
        state = jnp.exp(step_row[None, :] * rate) * state + (step_row * conv_row)[None, :] * in_row[:, None]
        return state, jnp.sum(out_row[:, None] * state, axis=0)

    start = jnp.zeros(rate.shape, jnp.float32)
    final, read = lax.scan(advance, start, (step, conv, state_in, state_out))
    mamba_out = ((read + skip_gain[None, :] * conv) * jax.nn.silu(inner_gate.astype(jnp.float32))).astype(jnp.bfloat16)

    length = query_heads.shape[0]
    kv_count = key_heads.shape[1] // HEAD_DIM
    q_count = query_heads.shape[1] // HEAD_DIM
    group = q_count // kv_count
    queries = query_heads.reshape(length, kv_count, group, HEAD_DIM).transpose(1, 2, 0, 3)
    keys = key_heads.reshape(length, kv_count, HEAD_DIM).transpose(1, 0, 2)
    values = value_heads.reshape(length, kv_count, HEAD_DIM).transpose(1, 0, 2)
    scale = HEAD_DIM ** -0.5
    rows = jnp.arange(length)
    allowed = rows[:, None] >= rows[None, :]

    def single_group(inputs):
        q_part, k_part, v_part = inputs
        scores = jnp.einsum("gld,md->glm", q_part.astype(jnp.float32), k_part.astype(jnp.float32)) * scale
        masked = jnp.where(allowed[None], scores, -1e30)
        peak = jnp.max(masked, axis=-1, keepdims=True)
        expo = jnp.where(allowed[None], jnp.exp(masked - peak), 0.0)
        total = jnp.sum(expo, axis=-1)
        weights = expo.astype(jnp.bfloat16)
        summed = jnp.einsum("glm,md->gld", weights.astype(jnp.float32), v_part.astype(jnp.float32))
        return summed / total[:, :, None]

    outs = lax.map(single_group, (queries, keys, values))
    attention_out = outs.transpose(2, 0, 1, 3).reshape(length, q_count * HEAD_DIM).astype(jnp.bfloat16)
    return (mamba_out, attention_out)
```

```python
import math

import jax
import jax.numpy as jnp
from jax import lax
from jax.sharding import PartitionSpec as P

HEAD_DIM = 128


def shifted(block, axis, distance):
    devices = range(lax.axis_size(axis))
    route = [(i - distance, i) for i in devices if i - distance in devices]
    return lax.ppermute(block, axis, route)


def convolve(padded, conv_weight, conv_bias):
    reach = conv_weight.shape[0] - 1
    length = padded.shape[0] - reach
    total = jnp.zeros((length, padded.shape[1]), jnp.float32)
    for index in range(reach + 1):
        total = total + conv_weight[index][None, :] * padded[index : index + length].astype(
            jnp.float32
        )
    return jax.nn.silu(total + conv_bias[None, :])


def attend_by_heads(q_three, k_three, v_three):
    tokens = q_three.shape[0]
    group = q_three.shape[1] // k_three.shape[1]
    k_wide = jnp.repeat(k_three, group, axis=1)
    v_wide = jnp.repeat(v_three, group, axis=1)
    q_all, k_all, v_all = (
        lax.all_to_all(q_three, "seq", split_axis=1, concat_axis=0, tiled=True),
        lax.all_to_all(k_wide, "seq", split_axis=1, concat_axis=0, tiled=True),
        lax.all_to_all(v_wide, "seq", split_axis=1, concat_axis=0, tiled=True),
    )
    length = q_all.shape[0]
    width = math.gcd(length, 512)
    scale = HEAD_DIM ** (-0.5)
    columns = jnp.arange(length)

    def block(index):
        start = index * width
        query_block = lax.dynamic_slice_in_dim(q_all, start, width, 0)
        scores = (
            jnp.einsum("ihd,jhd->hij", query_block, k_all, preferred_element_type=jnp.float32)
            * scale
        )
        rows = start + jnp.arange(width)
        allowed = rows[:, None] >= columns[None, :]
        masked = jnp.where(allowed[None], scores, -1e30)
        peak = jnp.max(masked, axis=-1, keepdims=True)
        expo = jnp.where(allowed[None], jnp.exp(masked - peak), 0.0)
        total = jnp.sum(expo, axis=-1)
        summed = jnp.einsum(
            "hij,jhd->ihd", expo.astype(jnp.bfloat16), v_all, preferred_element_type=jnp.float32
        )
        return (summed / jnp.transpose(total)[:, :, None]).astype(jnp.bfloat16)

    blocks = lax.map(block, jnp.arange(length // width))
    merged = blocks.reshape(length, q_all.shape[1], HEAD_DIM)
    back = lax.all_to_all(merged, "seq", split_axis=0, concat_axis=1, tiled=True)
    return back.reshape(tokens, -1)


def per_device(
    inner_x,
    inner_gate,
    conv_weight,
    conv_bias,
    step_low,
    step_proj,
    step_bias,
    decay_log,
    state_in,
    state_out,
    skip_gain,
    query_heads,
    key_heads,
    value_heads,
):
    reach = conv_weight.shape[0] - 1
    rim = shifted(inner_x[-reach:], "seq", 1)
    conv = convolve(jnp.concatenate([rim, inner_x], 0), conv_weight, conv_bias)
    step = jax.nn.softplus(
        jnp.dot(step_low, step_proj, preferred_element_type=jnp.float32) + step_bias[None, :]
    )
    rate = -jnp.exp(decay_log)

    def carry_only(state, row):
        step_row, conv_row, in_row = row
        state = (
            jnp.exp(step_row[None, :] * rate) * state
            + (step_row * conv_row)[None, :] * in_row[:, None]
        )
        return (state, None)

    def with_read(state, row):
        step_row, conv_row, in_row, out_row = row
        state = (
            jnp.exp(step_row[None, :] * rate) * state
            + (step_row * conv_row)[None, :] * in_row[:, None]
        )
        return (state, jnp.sum(out_row[:, None] * state, axis=0))

    zero_state = jnp.zeros(rate.shape, jnp.float32)
    local_end, unused = lax.scan(carry_only, zero_state, (step, conv, state_in), unroll=8)
    step_sum = jnp.sum(step, axis=0)[None, :]
    packed = shifted(jnp.concatenate([step_sum, local_end], 0), "seq", 1)
    distance = 1
    while distance < lax.axis_size("seq"):
        other = shifted(packed, "seq", distance)
        decay = jnp.exp(rate * packed[:1])
        packed = jnp.concatenate(
            [packed[:1] + other[:1], decay * other[1:] + packed[1:]], 0
        )
        distance *= 2
    incoming = packed[1:]
    final, read = lax.scan(with_read, incoming, (step, conv, state_in, state_out), unroll=8)
    mamba_out = (
        (read + skip_gain[None, :] * conv) * jax.nn.silu(inner_gate.astype(jnp.float32))
    ).astype(jnp.bfloat16)
    tokens = query_heads.shape[0]
    q_three = query_heads.reshape(tokens, -1, HEAD_DIM)
    k_three = key_heads.reshape(tokens, -1, HEAD_DIM)
    v_three = value_heads.reshape(tokens, -1, HEAD_DIM)
    attention_out = attend_by_heads(q_three, k_three, v_three)
    return (mamba_out, attention_out)


def solution(mesh):
    in_specs = (
        P(("stream", "seq"), None),
        P(("stream", "seq"), None),
        P(),
        P(),
        P(("stream", "seq"), None),
        P(),
        P(),
        P(),
        P(("stream", "seq"), None),
        P(("stream", "seq"), None),
        P(),
        P(("stream", "seq"), None),
        P(("stream", "seq"), None),
        P(("stream", "seq"), None),
    )
    out_specs = (P(("stream", "seq"), None), P(("stream", "seq"), None))
    return jax.shard_map(
        per_device, mesh=mesh, in_specs=in_specs, out_specs=out_specs, check_vma=False
    )
```

```python
import functools
import math

import jax
import jax.numpy as jnp
from jax import lax
from jax.experimental import pallas as pl
from jax.sharding import PartitionSpec as P

HEAD_DIM = 128
LANES = 128
CHANNEL_BLOCK = 512
INTERPRET = False


def shifted(block, axis, distance):
    devices = range(lax.axis_size(axis))
    route = [(i - distance, i) for i in devices if i - distance in devices]
    return lax.ppermute(block, axis, route)


def convolve(padded, conv_weight, conv_bias):
    reach = conv_weight.shape[0] - 1
    length = padded.shape[0] - reach
    total = jnp.zeros((length, padded.shape[1]), jnp.float32)
    for index in range(reach + 1):
        total = total + conv_weight[index][None, :] * padded[index : index + length].astype(
            jnp.float32
        )
    return jax.nn.silu(total + conv_bias[None, :])


def attend_by_heads(q_three, k_three, v_three):
    tokens = q_three.shape[0]
    group = q_three.shape[1] // k_three.shape[1]
    k_wide = jnp.repeat(k_three, group, axis=1)
    v_wide = jnp.repeat(v_three, group, axis=1)
    q_all, k_all, v_all = (
        lax.all_to_all(q_three, "seq", split_axis=1, concat_axis=0, tiled=True),
        lax.all_to_all(k_wide, "seq", split_axis=1, concat_axis=0, tiled=True),
        lax.all_to_all(v_wide, "seq", split_axis=1, concat_axis=0, tiled=True),
    )
    length = q_all.shape[0]
    width = math.gcd(length, 512)
    scale = HEAD_DIM ** (-0.5)
    columns = jnp.arange(length)

    pieces = []
    for index in range(length // width):
        stop = (index + 1) * width
        query_block = q_all[stop - width : stop]
        scores = (
            jnp.einsum(
                "ihd,jhd->hij", query_block, k_all[:stop], preferred_element_type=jnp.float32
            )
            * scale
        )
        rows = stop - width + jnp.arange(width)
        allowed = rows[:, None] >= columns[None, :stop]
        masked = jnp.where(allowed[None], scores, -1e30)
        peak = jnp.max(masked, axis=-1, keepdims=True)
        expo = jnp.where(allowed[None], jnp.exp(masked - peak), 0.0)
        total = jnp.sum(expo, axis=-1)
        summed = jnp.einsum(
            "hij,jhd->ihd",
            expo.astype(jnp.bfloat16),
            v_all[:stop],
            preferred_element_type=jnp.float32,
        )
        pieces.append((summed / jnp.transpose(total)[:, :, None]).astype(jnp.bfloat16))
    merged = jnp.concatenate(pieces, 0)
    back = lax.all_to_all(merged, "seq", split_axis=0, concat_axis=1, tiled=True)
    return back.reshape(tokens, -1)


def scan_kernel(step_ref, drive_ref, rate_ref, in_ref, out_ref, init_ref, result_ref, *, with_read):
    length = step_ref.shape[0]
    chunks = step_ref.shape[1] // LANES

    def body(i, states):
        first = pl.multiple_of(i * 8, 8)
        steps = [step_ref[pl.ds(first, 8), pl.ds(c * LANES, LANES)] for c in range(chunks)]
        drives = [drive_ref[pl.ds(first, 8), pl.ds(c * LANES, LANES)] for c in range(chunks)]
        reads = [[] for c in range(chunks)]
        for r in range(8):
            in_col = in_ref[first + r]
            out_col = out_ref[first + r]
            updated = []
            for c in range(chunks):
                decay = jnp.exp(steps[c][r : r + 1] * rate_ref[:, pl.ds(c * LANES, LANES)])
                state = decay * states[c] + drives[c][r : r + 1] * in_col
                updated.append(state)
                if with_read:
                    reads[c].append(jnp.sum(out_col * state, axis=0, keepdims=True))
            states = tuple(updated)
        if with_read:
            for c in range(chunks):
                result_ref[pl.ds(first, 8), pl.ds(c * LANES, LANES)] = jnp.concatenate(reads[c], 0)
        return states

    states = tuple(init_ref[:, pl.ds(c * LANES, LANES)] for c in range(chunks))
    states = lax.fori_loop(0, length // 8, body, states)
    if not with_read:
        for c in range(chunks):
            result_ref[:, pl.ds(c * LANES, LANES)] = states[c]


def run_scan(step, drive, rate, in_wide, out_wide, init, with_read):
    length, channels = step.shape
    entries = rate.shape[0]
    rows_spec = pl.BlockSpec((length, CHANNEL_BLOCK), lambda j: (0, j))
    state_spec = pl.BlockSpec((entries, CHANNEL_BLOCK), lambda j: (0, j))
    wide_spec = pl.BlockSpec((length, entries, LANES), lambda j: (0, 0, 0))
    shape = (length, channels) if with_read else (entries, channels)
    return pl.pallas_call(
        functools.partial(scan_kernel, with_read=with_read),
        grid=(channels // CHANNEL_BLOCK,),
        in_specs=[rows_spec, rows_spec, state_spec, wide_spec, wide_spec, state_spec],
        out_specs=rows_spec if with_read else state_spec,
        out_shape=jax.ShapeDtypeStruct(shape, jnp.float32),
        interpret=INTERPRET,
    )(step, drive, rate, in_wide, out_wide, init)


def exchange(step_sum, local_end, rate):
    count = lax.axis_size("seq")
    entries, channels = local_end.shape
    width = channels // count
    packed = jnp.concatenate([step_sum[None], local_end], 0).reshape(entries + 1, count, width)
    gathered = lax.all_to_all(packed, "seq", 1, 1, tiled=True)
    sums = gathered[0]
    ends = jnp.transpose(gathered[1:], (1, 0, 2))
    me = lax.axis_index("seq")
    rate_block = lax.dynamic_slice_in_dim(rate, me * width, width, 1)
    place = jnp.arange(count)
    between = (place[None, :, None] < place[None, None, :]) & (
        place[None, None, :] < place[:, None, None]
    )
    gap = jnp.sum(jnp.where(between[..., None], sums[None, None], 0.0), axis=2)
    before = place[None, :] < place[:, None]
    weight = jnp.where(
        before[:, :, None, None], jnp.exp(rate_block[None, None] * gap[:, :, None, :]), 0.0
    )
    incoming = jnp.sum(weight * ends[None], axis=1)
    back = lax.all_to_all(jnp.transpose(incoming, (1, 0, 2)), "seq", 1, 1, tiled=True)
    return back.reshape(entries, channels)


def per_device(
    inner_x,
    inner_gate,
    conv_weight,
    conv_bias,
    step_low,
    step_proj,
    step_bias,
    decay_log,
    state_in,
    state_out,
    skip_gain,
    query_heads,
    key_heads,
    value_heads,
):
    reach = conv_weight.shape[0] - 1
    rim = shifted(inner_x[-reach:], "seq", 1)
    conv = convolve(jnp.concatenate([rim, inner_x], 0), conv_weight, conv_bias)
    step = jax.nn.softplus(
        jnp.dot(step_low, step_proj, preferred_element_type=jnp.float32) + step_bias[None, :]
    )
    rate = -jnp.exp(decay_log)
    drive = step * conv
    length, entries = state_in.shape
    in_wide = jnp.broadcast_to(state_in[:, :, None], (length, entries, LANES))
    out_wide = jnp.broadcast_to(state_out[:, :, None], (length, entries, LANES))
    zero_state = jnp.zeros(rate.shape, jnp.float32)
    local_end = run_scan(step, drive, rate, in_wide, out_wide, zero_state, False)
    incoming = exchange(jnp.sum(step, axis=0), local_end, rate)
    read = run_scan(step, drive, rate, in_wide, out_wide, incoming, True)
    mamba_out = (
        (read + skip_gain[None, :] * conv) * jax.nn.silu(inner_gate.astype(jnp.float32))
    ).astype(jnp.bfloat16)
    tokens = query_heads.shape[0]
    q_three = query_heads.reshape(tokens, -1, HEAD_DIM)
    k_three = key_heads.reshape(tokens, -1, HEAD_DIM)
    v_three = value_heads.reshape(tokens, -1, HEAD_DIM)
    attention_out = attend_by_heads(q_three, k_three, v_three)
    return (mamba_out, attention_out)


def solution(mesh):
    in_specs = (
        P(("stream", "seq"), None),
        P(("stream", "seq"), None),
        P(),
        P(),
        P(("stream", "seq"), None),
        P(),
        P(),
        P(),
        P(("stream", "seq"), None),
        P(("stream", "seq"), None),
        P(),
        P(("stream", "seq"), None),
        P(("stream", "seq"), None),
        P(("stream", "seq"), None),
    )
    out_specs = (P(("stream", "seq"), None), P(("stream", "seq"), None))
    return jax.shard_map(
        per_device, mesh=mesh, in_specs=in_specs, out_specs=out_specs, check_vma=False
    )
```

```python
import functools
import math

import jax
import jax.numpy as jnp
from jax import lax
from jax.experimental import pallas as pl
from jax.sharding import PartitionSpec as P

HEAD_DIM = 128
LANES = 128
CHANNEL_BLOCK = 512
INTERPRET = False


def shifted(block, axis, distance):
    devices = range(lax.axis_size(axis))
    route = [(i - distance, i) for i in devices if i - distance in devices]
    return lax.ppermute(block, axis, route)


def convolve(padded, conv_weight, conv_bias):
    reach = conv_weight.shape[0] - 1
    length = padded.shape[0] - reach
    total = jnp.zeros((length, padded.shape[1]), jnp.float32)
    for index in range(reach + 1):
        total = total + conv_weight[index][None, :] * padded[index : index + length].astype(
            jnp.float32
        )
    return jax.nn.silu(total + conv_bias[None, :])


def attend_by_heads(q_three, k_three, v_three):
    tokens = q_three.shape[0]
    group = q_three.shape[1] // k_three.shape[1]
    k_wide = jnp.repeat(k_three, group, axis=1)
    v_wide = jnp.repeat(v_three, group, axis=1)
    joined = lax.all_to_all(
        jnp.concatenate([q_three, k_wide, v_wide], 2), "seq", split_axis=1, concat_axis=0, tiled=True
    )
    q_all = joined[:, :, :HEAD_DIM]
    k_all = joined[:, :, HEAD_DIM : 2 * HEAD_DIM]
    v_all = joined[:, :, 2 * HEAD_DIM :]
    length = q_all.shape[0]
    width = math.gcd(length, 512)
    scale = HEAD_DIM ** (-0.5)
    columns = jnp.arange(length)

    pieces = []
    for index in range(length // width):
        stop = (index + 1) * width
        query_block = q_all[stop - width : stop]
        scores = (
            jnp.einsum(
                "ihd,jhd->hij", query_block, k_all[:stop], preferred_element_type=jnp.float32
            )
            * scale
        )
        rows = stop - width + jnp.arange(width)
        allowed = rows[:, None] >= columns[None, :stop]
        masked = jnp.where(allowed[None], scores, -1e30)
        peak = jnp.max(masked, axis=-1, keepdims=True)
        expo = jnp.where(allowed[None], jnp.exp(masked - peak), 0.0)
        total = jnp.sum(expo, axis=-1)
        summed = jnp.einsum(
            "hij,jhd->ihd",
            expo.astype(jnp.bfloat16),
            v_all[:stop],
            preferred_element_type=jnp.float32,
        )
        pieces.append((summed / jnp.transpose(total)[:, :, None]).astype(jnp.bfloat16))
    merged = jnp.concatenate(pieces, 0)
    back = lax.all_to_all(merged, "seq", split_axis=0, concat_axis=1, tiled=True)
    return back.reshape(tokens, -1)


def scan_kernel(step_ref, drive_ref, rate_ref, in_ref, out_ref, init_ref, result_ref, *, with_read):
    length = step_ref.shape[0]
    chunks = step_ref.shape[1] // LANES

    def body(i, states):
        first = pl.multiple_of(i * 8, 8)
        steps = [step_ref[pl.ds(first, 8), pl.ds(c * LANES, LANES)] for c in range(chunks)]
        drives = [drive_ref[pl.ds(first, 8), pl.ds(c * LANES, LANES)] for c in range(chunks)]
        reads = [[] for c in range(chunks)]
        for r in range(8):
            in_col = in_ref[first + r]
            out_col = out_ref[first + r]
            updated = []
            for c in range(chunks):
                decay = jnp.exp(steps[c][r : r + 1] * rate_ref[:, pl.ds(c * LANES, LANES)])
                state = decay * states[c] + drives[c][r : r + 1] * in_col
                updated.append(state)
                if with_read:
                    reads[c].append(jnp.sum(out_col * state, axis=0, keepdims=True))
            states = tuple(updated)
        if with_read:
            for c in range(chunks):
                result_ref[pl.ds(first, 8), pl.ds(c * LANES, LANES)] = jnp.concatenate(reads[c], 0)
        return states

    states = tuple(init_ref[:, pl.ds(c * LANES, LANES)] for c in range(chunks))
    states = lax.fori_loop(0, length // 8, body, states)
    if not with_read:
        for c in range(chunks):
            result_ref[:, pl.ds(c * LANES, LANES)] = states[c]


def run_scan(step, drive, rate, in_wide, out_wide, init, with_read):
    length, channels = step.shape
    entries = rate.shape[0]
    rows_spec = pl.BlockSpec((length, CHANNEL_BLOCK), lambda j: (0, j))
    state_spec = pl.BlockSpec((entries, CHANNEL_BLOCK), lambda j: (0, j))
    wide_spec = pl.BlockSpec((length, entries, LANES), lambda j: (0, 0, 0))
    shape = (length, channels) if with_read else (entries, channels)
    return pl.pallas_call(
        functools.partial(scan_kernel, with_read=with_read),
        grid=(channels // CHANNEL_BLOCK,),
        in_specs=[rows_spec, rows_spec, state_spec, wide_spec, wide_spec, state_spec],
        out_specs=rows_spec if with_read else state_spec,
        out_shape=jax.ShapeDtypeStruct(shape, jnp.float32),
        interpret=INTERPRET,
    )(step, drive, rate, in_wide, out_wide, init)


def exchange(step_sum, local_end, rate):
    count = lax.axis_size("seq")
    entries, channels = local_end.shape
    width = channels // count
    packed = jnp.concatenate([step_sum[None], local_end], 0).reshape(entries + 1, count, width)
    gathered = lax.all_to_all(packed, "seq", 1, 1, tiled=True)
    sums = gathered[0]
    ends = jnp.transpose(gathered[1:], (1, 0, 2))
    me = lax.axis_index("seq")
    rate_block = lax.dynamic_slice_in_dim(rate, me * width, width, 1)
    place = jnp.arange(count)
    between = (place[None, :, None] < place[None, None, :]) & (
        place[None, None, :] < place[:, None, None]
    )
    gap = jnp.sum(jnp.where(between[..., None], sums[None, None], 0.0), axis=2)
    before = place[None, :] < place[:, None]
    weight = jnp.where(
        before[:, :, None, None], jnp.exp(rate_block[None, None] * gap[:, :, None, :]), 0.0
    )
    incoming = jnp.sum(weight * ends[None], axis=1)
    back = lax.all_to_all(jnp.transpose(incoming, (1, 0, 2)), "seq", 1, 1, tiled=True)
    return back.reshape(entries, channels)


def per_device(
    inner_x,
    inner_gate,
    conv_weight,
    conv_bias,
    step_low,
    step_proj,
    step_bias,
    decay_log,
    state_in,
    state_out,
    skip_gain,
    query_heads,
    key_heads,
    value_heads,
):
    reach = conv_weight.shape[0] - 1
    rim = shifted(inner_x[-reach:], "seq", 1)
    conv = convolve(jnp.concatenate([rim, inner_x], 0), conv_weight, conv_bias)
    step = jax.nn.softplus(
        jnp.dot(step_low, step_proj, preferred_element_type=jnp.float32) + step_bias[None, :]
    )
    rate = -jnp.exp(decay_log)
    drive = step * conv
    length, entries = state_in.shape
    in_wide = jnp.broadcast_to(state_in[:, :, None], (length, entries, LANES))
    out_wide = jnp.broadcast_to(state_out[:, :, None], (length, entries, LANES))
    zero_state = jnp.zeros(rate.shape, jnp.float32)
    local_end = run_scan(step, drive, rate, in_wide, out_wide, zero_state, False)
    incoming = exchange(jnp.sum(step, axis=0), local_end, rate)
    read = run_scan(step, drive, rate, in_wide, out_wide, incoming, True)
    mamba_out = (
        (read + skip_gain[None, :] * conv) * jax.nn.silu(inner_gate.astype(jnp.float32))
    ).astype(jnp.bfloat16)
    tokens = query_heads.shape[0]
    q_three = query_heads.reshape(tokens, -1, HEAD_DIM)
    k_three = key_heads.reshape(tokens, -1, HEAD_DIM)
    v_three = value_heads.reshape(tokens, -1, HEAD_DIM)
    attention_out = attend_by_heads(q_three, k_three, v_three)
    return (mamba_out, attention_out)


def solution(mesh):
    in_specs = (
        P(("stream", "seq"), None),
        P(("stream", "seq"), None),
        P(),
        P(),
        P(("stream", "seq"), None),
        P(),
        P(),
        P(),
        P(("stream", "seq"), None),
        P(("stream", "seq"), None),
        P(),
        P(("stream", "seq"), None),
        P(("stream", "seq"), None),
        P(("stream", "seq"), None),
    )
    out_specs = (P(("stream", "seq"), None), P(("stream", "seq"), None))
    return jax.shard_map(
        per_device, mesh=mesh, in_specs=in_specs, out_specs=out_specs, check_vma=False
    )
```

```python
import functools
import math

import jax
import jax.numpy as jnp
from jax import lax
from jax.experimental import pallas as pl
from jax.sharding import PartitionSpec as P

HEAD_DIM = 128
LANES = 128
CHANNEL_BLOCK = 512
INTERPRET = False


def shifted(block, axis, distance):
    devices = range(lax.axis_size(axis))
    route = [(i - distance, i) for i in devices if i - distance in devices]
    return lax.ppermute(block, axis, route)


def convolve(padded, conv_weight, conv_bias):
    reach = conv_weight.shape[0] - 1
    length = padded.shape[0] - reach
    total = jnp.zeros((length, padded.shape[1]), jnp.float32)
    for index in range(reach + 1):
        total = total + conv_weight[index][None, :] * padded[index : index + length].astype(
            jnp.float32
        )
    return jax.nn.silu(total + conv_bias[None, :])


def send_heads(q_three, k_three, v_three):
    group = q_three.shape[1] // k_three.shape[1]
    k_wide = jnp.repeat(k_three, group, axis=1)
    v_wide = jnp.repeat(v_three, group, axis=1)
    return lax.all_to_all(
        jnp.concatenate([q_three, k_wide, v_wide], 2), "seq", split_axis=1, concat_axis=0, tiled=True
    )


def attend_by_heads(joined, tokens):
    q_all = joined[:, :, :HEAD_DIM]
    k_all = joined[:, :, HEAD_DIM : 2 * HEAD_DIM]
    v_all = joined[:, :, 2 * HEAD_DIM :]
    length = q_all.shape[0]
    width = math.gcd(length, 512)
    scale = HEAD_DIM ** (-0.5)
    columns = jnp.arange(length)

    pieces = []
    for index in range(length // width):
        stop = (index + 1) * width
        query_block = q_all[stop - width : stop]
        scores = (
            jnp.einsum(
                "ihd,jhd->hij", query_block, k_all[:stop], preferred_element_type=jnp.float32
            )
            * scale
        )
        rows = stop - width + jnp.arange(width)
        allowed = rows[:, None] >= columns[None, :stop]
        masked = jnp.where(allowed[None], scores, -1e30)
        peak = jnp.max(masked, axis=-1, keepdims=True)
        expo = jnp.where(allowed[None], jnp.exp(masked - peak), 0.0)
        total = jnp.sum(expo, axis=-1)
        summed = jnp.einsum(
            "hij,jhd->ihd",
            expo.astype(jnp.bfloat16),
            v_all[:stop],
            preferred_element_type=jnp.float32,
        )
        pieces.append((summed / jnp.transpose(total)[:, :, None]).astype(jnp.bfloat16))
    merged = jnp.concatenate(pieces, 0)
    back = lax.all_to_all(merged, "seq", split_axis=0, concat_axis=1, tiled=True)
    return back.reshape(tokens, -1)


def scan_kernel(step_ref, drive_ref, rate_ref, in_ref, out_ref, init_ref, result_ref, *, with_read):
    length = step_ref.shape[0]
    chunks = step_ref.shape[1] // LANES

    def body(i, states):
        first = pl.multiple_of(i * 8, 8)
        steps = [step_ref[pl.ds(first, 8), pl.ds(c * LANES, LANES)] for c in range(chunks)]
        drives = [drive_ref[pl.ds(first, 8), pl.ds(c * LANES, LANES)] for c in range(chunks)]
        reads = [[] for c in range(chunks)]
        for r in range(8):
            in_col = in_ref[first + r]
            out_col = out_ref[first + r]
            updated = []
            for c in range(chunks):
                decay = jnp.exp(steps[c][r : r + 1] * rate_ref[:, pl.ds(c * LANES, LANES)])
                state = decay * states[c] + drives[c][r : r + 1] * in_col
                updated.append(state)
                if with_read:
                    reads[c].append(jnp.sum(out_col * state, axis=0, keepdims=True))
            states = tuple(updated)
        if with_read:
            for c in range(chunks):
                result_ref[pl.ds(first, 8), pl.ds(c * LANES, LANES)] = jnp.concatenate(reads[c], 0)
        return states

    states = tuple(init_ref[:, pl.ds(c * LANES, LANES)] for c in range(chunks))
    states = lax.fori_loop(0, length // 8, body, states)
    if not with_read:
        for c in range(chunks):
            result_ref[:, pl.ds(c * LANES, LANES)] = states[c]


def run_scan(step, drive, rate, in_wide, out_wide, init, with_read):
    length, channels = step.shape
    entries = rate.shape[0]
    rows_spec = pl.BlockSpec((length, CHANNEL_BLOCK), lambda j: (0, j))
    state_spec = pl.BlockSpec((entries, CHANNEL_BLOCK), lambda j: (0, j))
    wide_spec = pl.BlockSpec((length, entries, LANES), lambda j: (0, 0, 0))
    shape = (length, channels) if with_read else (entries, channels)
    return pl.pallas_call(
        functools.partial(scan_kernel, with_read=with_read),
        grid=(channels // CHANNEL_BLOCK,),
        in_specs=[rows_spec, rows_spec, state_spec, wide_spec, wide_spec, state_spec],
        out_specs=rows_spec if with_read else state_spec,
        out_shape=jax.ShapeDtypeStruct(shape, jnp.float32),
        interpret=INTERPRET,
    )(step, drive, rate, in_wide, out_wide, init)


def exchange(step_sum, local_end, rate, joined):
    count = lax.axis_size("seq")
    entries, channels = local_end.shape
    width = channels // count
    packed = jnp.concatenate([step_sum[None], local_end], 0).reshape(entries + 1, count, width)
    packed, joined = lax.optimization_barrier((packed, joined))
    gathered = lax.all_to_all(packed, "seq", 1, 1, tiled=True)
    sums = gathered[0]
    ends = jnp.transpose(gathered[1:], (1, 0, 2))
    me = lax.axis_index("seq")
    rate_block = lax.dynamic_slice_in_dim(rate, me * width, width, 1)
    place = jnp.arange(count)
    between = (place[None, :, None] < place[None, None, :]) & (
        place[None, None, :] < place[:, None, None]
    )
    gap = jnp.sum(jnp.where(between[..., None], sums[None, None], 0.0), axis=2)
    before = place[None, :] < place[:, None]
    weight = jnp.where(
        before[:, :, None, None], jnp.exp(rate_block[None, None] * gap[:, :, None, :]), 0.0
    )
    incoming = jnp.sum(weight * ends[None], axis=1)
    back = lax.all_to_all(jnp.transpose(incoming, (1, 0, 2)), "seq", 1, 1, tiled=True)
    return back.reshape(entries, channels), joined


def per_device(
    inner_x,
    inner_gate,
    conv_weight,
    conv_bias,
    step_low,
    step_proj,
    step_bias,
    decay_log,
    state_in,
    state_out,
    skip_gain,
    query_heads,
    key_heads,
    value_heads,
):
    reach = conv_weight.shape[0] - 1
    rim = shifted(inner_x[-reach:], "seq", 1)
    conv = convolve(jnp.concatenate([rim, inner_x], 0), conv_weight, conv_bias)
    step = jax.nn.softplus(
        jnp.dot(step_low, step_proj, preferred_element_type=jnp.float32) + step_bias[None, :]
    )
    rate = -jnp.exp(decay_log)
    drive = step * conv
    length, entries = state_in.shape
    in_wide = jnp.broadcast_to(state_in[:, :, None], (length, entries, LANES))
    out_wide = jnp.broadcast_to(state_out[:, :, None], (length, entries, LANES))
    zero_state = jnp.zeros(rate.shape, jnp.float32)
    local_end = run_scan(step, drive, rate, in_wide, out_wide, zero_state, False)
    tokens = query_heads.shape[0]
    joined = send_heads(
        query_heads.reshape(tokens, -1, HEAD_DIM),
        key_heads.reshape(tokens, -1, HEAD_DIM),
        value_heads.reshape(tokens, -1, HEAD_DIM),
    )
    incoming, joined = exchange(jnp.sum(step, axis=0), local_end, rate, joined)
    read = run_scan(step, drive, rate, in_wide, out_wide, incoming, True)
    mamba_out = (
        (read + skip_gain[None, :] * conv) * jax.nn.silu(inner_gate.astype(jnp.float32))
    ).astype(jnp.bfloat16)
    attention_out = attend_by_heads(joined, tokens)
    return (mamba_out, attention_out)


def solution(mesh):
    in_specs = (
        P(("stream", "seq"), None),
        P(("stream", "seq"), None),
        P(),
        P(),
        P(("stream", "seq"), None),
        P(),
        P(),
        P(),
        P(("stream", "seq"), None),
        P(("stream", "seq"), None),
        P(),
        P(("stream", "seq"), None),
        P(("stream", "seq"), None),
        P(("stream", "seq"), None),
    )
    out_specs = (P(("stream", "seq"), None), P(("stream", "seq"), None))
    return jax.shard_map(
        per_device, mesh=mesh, in_specs=in_specs, out_specs=out_specs, check_vma=False
    )
```

```python
import functools
import math

import jax
import jax.numpy as jnp
from jax import lax
from jax.experimental import pallas as pl
from jax.sharding import PartitionSpec as P

HEAD_DIM = 128
LANES = 128
CHANNEL_BLOCK = 512
INTERPRET = False


def shifted(block, axis, distance):
    devices = range(lax.axis_size(axis))
    route = [(i - distance, i) for i in devices if i - distance in devices]
    return lax.ppermute(block, axis, route)


def convolve(padded, conv_weight, conv_bias):
    reach = conv_weight.shape[0] - 1
    length = padded.shape[0] - reach
    total = jnp.zeros((length, padded.shape[1]), jnp.float32)
    for index in range(reach + 1):
        total = total + conv_weight[index][None, :] * padded[index : index + length].astype(
            jnp.float32
        )
    return jax.nn.silu(total + conv_bias[None, :])


def send_heads(q_three, k_three, v_three):
    group = q_three.shape[1] // k_three.shape[1]
    k_wide = jnp.repeat(k_three, group, axis=1)
    v_wide = jnp.repeat(v_three, group, axis=1)
    return lax.all_to_all(
        jnp.concatenate([q_three, k_wide, v_wide], 2), "seq", split_axis=1, concat_axis=0, tiled=True
    )


def attend_by_heads(joined, tokens, midway):
    q_all = joined[:, :, :HEAD_DIM]
    k_all = joined[:, :, HEAD_DIM : 2 * HEAD_DIM]
    v_all = joined[:, :, 2 * HEAD_DIM :]
    length = q_all.shape[0]
    width = math.gcd(length, 512)
    scale = HEAD_DIM ** (-0.5)
    columns = jnp.arange(length)

    pieces = []
    for index in range(length // width):
        if index == length // width // 2:
            q_all, k_all, v_all = midway(q_all, k_all, v_all)
        stop = (index + 1) * width
        query_block = q_all[stop - width : stop]
        scores = (
            jnp.einsum(
                "ihd,jhd->hij", query_block, k_all[:stop], preferred_element_type=jnp.float32
            )
            * scale
        )
        rows = stop - width + jnp.arange(width)
        allowed = rows[:, None] >= columns[None, :stop]
        masked = jnp.where(allowed[None], scores, -1e30)
        peak = jnp.max(masked, axis=-1, keepdims=True)
        expo = jnp.where(allowed[None], jnp.exp(masked - peak), 0.0)
        total = jnp.sum(expo, axis=-1)
        summed = jnp.einsum(
            "hij,jhd->ihd",
            expo.astype(jnp.bfloat16),
            v_all[:stop],
            preferred_element_type=jnp.float32,
        )
        pieces.append((summed / jnp.transpose(total)[:, :, None]).astype(jnp.bfloat16))
    merged = jnp.concatenate(pieces, 0)
    back = lax.all_to_all(merged, "seq", split_axis=0, concat_axis=1, tiled=True)
    return back.reshape(tokens, -1)


def scan_kernel(step_ref, drive_ref, rate_ref, in_ref, out_ref, init_ref, result_ref, *, with_read):
    length = step_ref.shape[0]
    chunks = step_ref.shape[1] // LANES

    def body(i, states):
        first = pl.multiple_of(i * 8, 8)
        steps = [step_ref[pl.ds(first, 8), pl.ds(c * LANES, LANES)] for c in range(chunks)]
        drives = [drive_ref[pl.ds(first, 8), pl.ds(c * LANES, LANES)] for c in range(chunks)]
        reads = [[] for c in range(chunks)]
        for r in range(8):
            in_col = in_ref[first + r]
            out_col = out_ref[first + r]
            updated = []
            for c in range(chunks):
                decay = jnp.exp(steps[c][r : r + 1] * rate_ref[:, pl.ds(c * LANES, LANES)])
                state = decay * states[c] + drives[c][r : r + 1] * in_col
                updated.append(state)
                if with_read:
                    reads[c].append(jnp.sum(out_col * state, axis=0, keepdims=True))
            states = tuple(updated)
        if with_read:
            for c in range(chunks):
                result_ref[pl.ds(first, 8), pl.ds(c * LANES, LANES)] = jnp.concatenate(reads[c], 0)
        return states

    states = tuple(init_ref[:, pl.ds(c * LANES, LANES)] for c in range(chunks))
    states = lax.fori_loop(0, length // 8, body, states)
    if not with_read:
        for c in range(chunks):
            result_ref[:, pl.ds(c * LANES, LANES)] = states[c]


def run_scan(step, drive, rate, in_wide, out_wide, init, with_read):
    length, channels = step.shape
    entries = rate.shape[0]
    rows_spec = pl.BlockSpec((length, CHANNEL_BLOCK), lambda j: (0, j))
    state_spec = pl.BlockSpec((entries, CHANNEL_BLOCK), lambda j: (0, j))
    wide_spec = pl.BlockSpec((length, entries, LANES), lambda j: (0, 0, 0))
    shape = (length, channels) if with_read else (entries, channels)
    return pl.pallas_call(
        functools.partial(scan_kernel, with_read=with_read),
        grid=(channels // CHANNEL_BLOCK,),
        in_specs=[rows_spec, rows_spec, state_spec, wide_spec, wide_spec, state_spec],
        out_specs=rows_spec if with_read else state_spec,
        out_shape=jax.ShapeDtypeStruct(shape, jnp.float32),
        interpret=INTERPRET,
    )(step, drive, rate, in_wide, out_wide, init)


def exchange_send(step_sum, local_end, joined):
    count = lax.axis_size("seq")
    entries, channels = local_end.shape
    packed = jnp.concatenate([step_sum[None], local_end], 0).reshape(entries + 1, count, -1)
    packed, joined = lax.optimization_barrier((packed, joined))
    return lax.all_to_all(packed, "seq", 1, 1, tiled=True), joined


def exchange_prefix(gathered, rate):
    count, width = gathered.shape[1:]
    sums = gathered[0]
    ends = jnp.transpose(gathered[1:], (1, 0, 2))
    me = lax.axis_index("seq")
    rate_block = lax.dynamic_slice_in_dim(rate, me * width, width, 1)
    place = jnp.arange(count)
    between = (place[None, :, None] < place[None, None, :]) & (
        place[None, None, :] < place[:, None, None]
    )
    gap = jnp.sum(jnp.where(between[..., None], sums[None, None], 0.0), axis=2)
    before = place[None, :] < place[:, None]
    weight = jnp.where(
        before[:, :, None, None], jnp.exp(rate_block[None, None] * gap[:, :, None, :]), 0.0
    )
    return jnp.sum(weight * ends[None], axis=1)


def exchange_return(incoming):
    count, entries, width = incoming.shape
    back = lax.all_to_all(jnp.transpose(incoming, (1, 0, 2)), "seq", 1, 1, tiled=True)
    return back.reshape(entries, count * width)


def per_device(
    inner_x,
    inner_gate,
    conv_weight,
    conv_bias,
    step_low,
    step_proj,
    step_bias,
    decay_log,
    state_in,
    state_out,
    skip_gain,
    query_heads,
    key_heads,
    value_heads,
):
    reach = conv_weight.shape[0] - 1
    rim = shifted(inner_x[-reach:], "seq", 1)
    rim, query_heads, key_heads, value_heads = lax.optimization_barrier(
        (rim, query_heads, key_heads, value_heads)
    )
    conv = convolve(jnp.concatenate([rim, inner_x], 0), conv_weight, conv_bias)
    step = jax.nn.softplus(
        jnp.dot(step_low, step_proj, preferred_element_type=jnp.float32) + step_bias[None, :]
    )
    rate = -jnp.exp(decay_log)
    drive = step * conv
    length, entries = state_in.shape
    in_wide = jnp.broadcast_to(state_in[:, :, None], (length, entries, LANES))
    out_wide = jnp.broadcast_to(state_out[:, :, None], (length, entries, LANES))
    zero_state = jnp.zeros(rate.shape, jnp.float32)
    local_end = run_scan(step, drive, rate, in_wide, out_wide, zero_state, False)
    tokens = query_heads.shape[0]
    joined = send_heads(
        query_heads.reshape(tokens, -1, HEAD_DIM),
        key_heads.reshape(tokens, -1, HEAD_DIM),
        value_heads.reshape(tokens, -1, HEAD_DIM),
    )
    gathered, joined = exchange_send(jnp.sum(step, axis=0), local_end, joined)
    prefix = []

    def midway(q_all, k_all, v_all):
        prefix.append(exchange_prefix(gathered, rate))
        return lax.optimization_barrier((prefix[0], q_all, k_all, v_all))[1:]

    attention_out = attend_by_heads(joined, tokens, midway)
    incoming = exchange_return(prefix[0])
    read = run_scan(step, drive, rate, in_wide, out_wide, incoming, True)
    mamba_out = (
        (read + skip_gain[None, :] * conv) * jax.nn.silu(inner_gate.astype(jnp.float32))
    ).astype(jnp.bfloat16)
    return (mamba_out, attention_out)


def solution(mesh):
    in_specs = (
        P(("stream", "seq"), None),
        P(("stream", "seq"), None),
        P(),
        P(),
        P(("stream", "seq"), None),
        P(),
        P(),
        P(),
        P(("stream", "seq"), None),
        P(("stream", "seq"), None),
        P(),
        P(("stream", "seq"), None),
        P(("stream", "seq"), None),
        P(("stream", "seq"), None),
    )
    out_specs = (P(("stream", "seq"), None), P(("stream", "seq"), None))
    return jax.shard_map(
        per_device, mesh=mesh, in_specs=in_specs, out_specs=out_specs, check_vma=False
    )
```

```python
import functools
import math

import jax
import jax.numpy as jnp
from jax import lax
from jax.experimental import pallas as pl
from jax.sharding import PartitionSpec as P

HEAD_DIM = 128
LANES = 128
CHANNEL_BLOCK = 512
INTERPRET = False


def shifted(block, axis, distance):
    devices = range(lax.axis_size(axis))
    route = [(i - distance, i) for i in devices if i - distance in devices]
    return lax.ppermute(block, axis, route)


def convolve(padded, conv_weight, conv_bias):
    reach = conv_weight.shape[0] - 1
    length = padded.shape[0] - reach
    total = jnp.zeros((length, padded.shape[1]), jnp.float32)
    for index in range(reach + 1):
        total = total + conv_weight[index][None, :] * padded[index : index + length].astype(
            jnp.float32
        )
    return jax.nn.silu(total + conv_bias[None, :])


def send_heads(q_three, k_three, v_three):
    tokens, heads = q_three.shape[:2]
    count = lax.axis_size("seq")
    group = heads // k_three.shape[1]
    k_wide = jnp.repeat(k_three, group, axis=1)
    v_wide = jnp.repeat(v_three, group, axis=1)
    joined = jnp.concatenate([q_three, k_wide, v_wide], 2).reshape(tokens, count, heads // count, -1)
    arrived = lax.all_to_all(
        jnp.transpose(joined, (1, 0, 2, 3)), "seq", split_axis=0, concat_axis=0, tiled=True
    )
    return arrived.reshape(count * tokens, heads // count, -1)


def attend_by_heads(joined, tokens, midway):
    q_all = joined[:, :, :HEAD_DIM]
    k_all = joined[:, :, HEAD_DIM : 2 * HEAD_DIM]
    v_all = joined[:, :, 2 * HEAD_DIM :]
    length = q_all.shape[0]
    width = math.gcd(length, 512)
    scale = HEAD_DIM ** (-0.5)
    columns = jnp.arange(length)

    pieces = []
    for index in range(length // width):
        if index == length // width // 2:
            q_all, k_all, v_all = midway(q_all, k_all, v_all)
        stop = (index + 1) * width
        query_block = q_all[stop - width : stop]
        scores = (
            jnp.einsum(
                "ihd,jhd->hij", query_block, k_all[:stop], preferred_element_type=jnp.float32
            )
            * scale
        )
        rows = stop - width + jnp.arange(width)
        allowed = rows[:, None] >= columns[None, :stop]
        masked = jnp.where(allowed[None], scores, -1e30)
        peak = jnp.max(masked, axis=-1, keepdims=True)
        expo = jnp.where(allowed[None], jnp.exp(masked - peak), 0.0)
        total = jnp.sum(expo, axis=-1)
        summed = jnp.einsum(
            "hij,jhd->ihd",
            expo.astype(jnp.bfloat16),
            v_all[:stop],
            preferred_element_type=jnp.float32,
        )
        pieces.append((summed / jnp.transpose(total)[:, :, None]).astype(jnp.bfloat16))
    merged = jnp.concatenate(pieces, 0)
    count = length // tokens
    back = lax.all_to_all(
        merged.reshape(count, tokens, -1), "seq", split_axis=0, concat_axis=0, tiled=True
    )
    return jnp.transpose(back, (1, 0, 2)).reshape(tokens, -1)


def scan_kernel(step_ref, drive_ref, rate_ref, in_ref, out_ref, init_ref, result_ref, *, with_read):
    length = step_ref.shape[0]
    chunks = step_ref.shape[1] // LANES

    def body(i, states):
        first = pl.multiple_of(i * 8, 8)
        steps = [step_ref[pl.ds(first, 8), pl.ds(c * LANES, LANES)] for c in range(chunks)]
        drives = [drive_ref[pl.ds(first, 8), pl.ds(c * LANES, LANES)] for c in range(chunks)]
        reads = [[] for c in range(chunks)]
        for r in range(8):
            in_col = in_ref[first + r]
            out_col = out_ref[first + r]
            updated = []
            for c in range(chunks):
                decay = jnp.exp(steps[c][r : r + 1] * rate_ref[:, pl.ds(c * LANES, LANES)])
                state = decay * states[c] + drives[c][r : r + 1] * in_col
                updated.append(state)
                if with_read:
                    reads[c].append(jnp.sum(out_col * state, axis=0, keepdims=True))
            states = tuple(updated)
        if with_read:
            for c in range(chunks):
                result_ref[pl.ds(first, 8), pl.ds(c * LANES, LANES)] = jnp.concatenate(reads[c], 0)
        return states

    states = tuple(init_ref[:, pl.ds(c * LANES, LANES)] for c in range(chunks))
    states = lax.fori_loop(0, length // 8, body, states)
    if not with_read:
        for c in range(chunks):
            result_ref[:, pl.ds(c * LANES, LANES)] = states[c]


def run_scan(step, drive, rate, in_wide, out_wide, init, with_read):
    length, channels = step.shape
    entries = rate.shape[0]
    rows_spec = pl.BlockSpec((length, CHANNEL_BLOCK), lambda j: (0, j))
    state_spec = pl.BlockSpec((entries, CHANNEL_BLOCK), lambda j: (0, j))
    wide_spec = pl.BlockSpec((length, entries, LANES), lambda j: (0, 0, 0))
    shape = (length, channels) if with_read else (entries, channels)
    return pl.pallas_call(
        functools.partial(scan_kernel, with_read=with_read),
        grid=(channels // CHANNEL_BLOCK,),
        in_specs=[rows_spec, rows_spec, state_spec, wide_spec, wide_spec, state_spec],
        out_specs=rows_spec if with_read else state_spec,
        out_shape=jax.ShapeDtypeStruct(shape, jnp.float32),
        interpret=INTERPRET,
    )(step, drive, rate, in_wide, out_wide, init)


def exchange_send(step_sum, local_end, joined):
    count = lax.axis_size("seq")
    entries, channels = local_end.shape
    packed = jnp.concatenate([step_sum[None], local_end], 0).reshape(entries + 1, count, -1)
    packed, joined = lax.optimization_barrier((packed, joined))
    return lax.all_to_all(packed, "seq", 1, 1, tiled=True), joined


def exchange_prefix(gathered, rate):
    count, width = gathered.shape[1:]
    sums = gathered[0]
    ends = jnp.transpose(gathered[1:], (1, 0, 2))
    me = lax.axis_index("seq")
    rate_block = lax.dynamic_slice_in_dim(rate, me * width, width, 1)
    place = jnp.arange(count)
    between = (place[None, :, None] < place[None, None, :]) & (
        place[None, None, :] < place[:, None, None]
    )
    gap = jnp.dot(
        between.reshape(count * count, count).astype(jnp.float32),
        sums,
        precision=lax.Precision.HIGHEST,
    ).reshape(count, count, width)
    before = place[None, :] < place[:, None]
    weight = jnp.where(
        before[:, :, None, None], jnp.exp(rate_block[None, None] * gap[:, :, None, :]), 0.0
    )
    return jnp.sum(weight * ends[None], axis=1)


def exchange_return(incoming):
    count, entries, width = incoming.shape
    back = lax.all_to_all(jnp.transpose(incoming, (1, 0, 2)), "seq", 1, 1, tiled=True)
    return back.reshape(entries, count * width)


def per_device(
    inner_x,
    inner_gate,
    conv_weight,
    conv_bias,
    step_low,
    step_proj,
    step_bias,
    decay_log,
    state_in,
    state_out,
    skip_gain,
    query_heads,
    key_heads,
    value_heads,
):
    reach = conv_weight.shape[0] - 1
    rim = shifted(inner_x[-reach:], "seq", 1)
    rim, query_heads, key_heads, value_heads = lax.optimization_barrier(
        (rim, query_heads, key_heads, value_heads)
    )
    conv = convolve(jnp.concatenate([rim, inner_x], 0), conv_weight, conv_bias)
    step = jax.nn.softplus(
        jnp.dot(step_low, step_proj, preferred_element_type=jnp.float32) + step_bias[None, :]
    )
    rate = -jnp.exp(decay_log)
    drive = step * conv
    length, entries = state_in.shape
    in_wide = jnp.broadcast_to(state_in[:, :, None], (length, entries, LANES))
    out_wide = jnp.broadcast_to(state_out[:, :, None], (length, entries, LANES))
    zero_state = jnp.zeros(rate.shape, jnp.float32)
    local_end = run_scan(step, drive, rate, in_wide, out_wide, zero_state, False)
    tokens = query_heads.shape[0]
    joined = send_heads(
        query_heads.reshape(tokens, -1, HEAD_DIM),
        key_heads.reshape(tokens, -1, HEAD_DIM),
        value_heads.reshape(tokens, -1, HEAD_DIM),
    )
    gathered, joined = exchange_send(jnp.sum(step, axis=0), local_end, joined)
    prefix = []

    def midway(q_all, k_all, v_all):
        prefix.append(exchange_prefix(gathered, rate))
        return lax.optimization_barrier((prefix[0], q_all, k_all, v_all))[1:]

    attention_out = attend_by_heads(joined, tokens, midway)
    incoming = exchange_return(prefix[0])
    read = run_scan(step, drive, rate, in_wide, out_wide, incoming, True)
    mamba_out = (
        (read + skip_gain[None, :] * conv) * jax.nn.silu(inner_gate.astype(jnp.float32))
    ).astype(jnp.bfloat16)
    return (mamba_out, attention_out)


def solution(mesh):
    in_specs = (
        P(("stream", "seq"), None),
        P(("stream", "seq"), None),
        P(),
        P(),
        P(("stream", "seq"), None),
        P(),
        P(),
        P(),
        P(("stream", "seq"), None),
        P(("stream", "seq"), None),
        P(),
        P(("stream", "seq"), None),
        P(("stream", "seq"), None),
        P(("stream", "seq"), None),
    )
    out_specs = (P(("stream", "seq"), None), P(("stream", "seq"), None))
    return jax.shard_map(
        per_device, mesh=mesh, in_specs=in_specs, out_specs=out_specs, check_vma=False
    )
```

```python
import functools
import math

import jax
import jax.numpy as jnp
from jax import lax
from jax.experimental import pallas as pl
from jax.sharding import PartitionSpec as P

HEAD_DIM = 128
LANES = 128
CHANNEL_BLOCK = 512
INTERPRET = False


def shifted(block, axis, distance):
    devices = range(lax.axis_size(axis))
    route = [(i - distance, i) for i in devices if i - distance in devices]
    return lax.ppermute(block, axis, route)


def convolve(padded, conv_weight, conv_bias):
    reach = conv_weight.shape[0] - 1
    length = padded.shape[0] - reach
    total = jnp.zeros((length, padded.shape[1]), jnp.float32)
    for index in range(reach + 1):
        total = total + conv_weight[index][None, :] * padded[index : index + length].astype(
            jnp.float32
        )
    return jax.nn.silu(total + conv_bias[None, :])


def send_heads(q_three, k_three, v_three):
    tokens, heads = q_three.shape[:2]
    count = lax.axis_size("seq")
    group = heads // k_three.shape[1]
    k_wide = jnp.repeat(k_three, group, axis=1)
    v_wide = jnp.repeat(v_three, group, axis=1)
    joined = jnp.concatenate([q_three, k_wide, v_wide], 2).reshape(tokens, count, heads // count, -1)
    arrived = lax.all_to_all(
        jnp.transpose(joined, (1, 0, 2, 3)), "seq", split_axis=0, concat_axis=0, tiled=True
    )
    return arrived.reshape(count * tokens, heads // count, -1)


def attention_kernel(q_ref, k_ref, v_ref, o_ref, *, tile, scale, first):
    index = pl.program_id(1) + first
    query = q_ref[0]
    rows = lax.broadcasted_iota(jnp.int32, (tile, tile), 0)
    cols = lax.broadcasted_iota(jnp.int32, (tile, tile), 1)
    diagonal = rows >= cols

    def scores(j):
        keys = k_ref[0, pl.ds(pl.multiple_of(j * tile, tile), tile), :]
        product = lax.dot_general(
            query, keys, (((1,), (1,)), ((), ())), preferred_element_type=jnp.float32
        )
        return product * scale

    def peak_step(j, peak):
        return jnp.maximum(peak, jnp.max(scores(j), axis=1, keepdims=True))

    peak = jnp.full((tile, 1), -jnp.inf, jnp.float32)
    peak = lax.fori_loop(0, index, peak_step, peak)
    last = jnp.where(diagonal, scores(index), -1e30)
    peak = jnp.maximum(peak, jnp.max(last, axis=1, keepdims=True))

    def add_block(j, expo, carry):
        total, summed = carry
        values = v_ref[0, pl.ds(pl.multiple_of(j * tile, tile), tile), :]
        summed = summed + lax.dot_general(
            expo.astype(jnp.bfloat16), values, (((1,), (0,)), ((), ())),
            preferred_element_type=jnp.float32,
        )
        return total + jnp.sum(expo, axis=1, keepdims=True), summed

    def sum_step(j, carry):
        return add_block(j, jnp.exp(scores(j) - peak), carry)

    carry = (jnp.zeros((tile, 1), jnp.float32), jnp.zeros((tile, HEAD_DIM), jnp.float32))
    carry = lax.fori_loop(0, index, sum_step, carry)
    expo = jnp.where(diagonal, jnp.exp(last - peak), 0.0)
    total, summed = add_block(index, expo, carry)
    o_ref[0] = (summed / total).astype(o_ref.dtype)


def attend_heads(q_all, k_all, v_all, first, blocks):
    heads, length, _ = q_all.shape
    tile = length // blocks
    head_spec = pl.BlockSpec((1, length, HEAD_DIM), lambda h, i: (h, 0, 0))
    tile_spec = pl.BlockSpec((1, tile, HEAD_DIM), lambda h, i: (h, i + first, 0))
    out_spec = pl.BlockSpec((1, tile, HEAD_DIM), lambda h, i: (h, i, 0))
    return pl.pallas_call(
        functools.partial(attention_kernel, tile=tile, scale=HEAD_DIM ** (-0.5), first=first),
        grid=(heads, blocks // 2),
        in_specs=[tile_spec, head_spec, head_spec],
        out_specs=out_spec,
        out_shape=jax.ShapeDtypeStruct((heads, length // 2, HEAD_DIM), jnp.bfloat16),
        interpret=INTERPRET,
    )(q_all, k_all, v_all)


def attend_by_heads(joined, tokens, midway):
    length = joined.shape[0]
    blocks = length // math.gcd(length, 512)
    heads_first = [jnp.transpose(x, (1, 0, 2)) for x in (
        joined[:, :, :HEAD_DIM], joined[:, :, HEAD_DIM : 2 * HEAD_DIM], joined[:, :, 2 * HEAD_DIM :]
    )]
    early, heads_first = midway(attend_heads(*heads_first, 0, blocks), heads_first)
    late = attend_heads(*heads_first, blocks // 2, blocks)
    merged = jnp.transpose(jnp.concatenate([early, late], 1), (1, 0, 2))
    length = merged.shape[0]
    count = length // tokens
    back = lax.all_to_all(
        merged.reshape(count, tokens, -1), "seq", split_axis=0, concat_axis=0, tiled=True
    )
    return jnp.transpose(back, (1, 0, 2)).reshape(tokens, -1)


def scan_kernel(step_ref, drive_ref, rate_ref, in_ref, out_ref, init_ref, result_ref, *, with_read):
    length = step_ref.shape[0]
    chunks = step_ref.shape[1] // LANES

    def body(i, states):
        first = pl.multiple_of(i * 8, 8)
        steps = [step_ref[pl.ds(first, 8), pl.ds(c * LANES, LANES)] for c in range(chunks)]
        drives = [drive_ref[pl.ds(first, 8), pl.ds(c * LANES, LANES)] for c in range(chunks)]
        reads = [[] for c in range(chunks)]
        for r in range(8):
            in_col = in_ref[first + r]
            out_col = out_ref[first + r]
            updated = []
            for c in range(chunks):
                decay = jnp.exp(steps[c][r : r + 1] * rate_ref[:, pl.ds(c * LANES, LANES)])
                state = decay * states[c] + drives[c][r : r + 1] * in_col
                updated.append(state)
                if with_read:
                    reads[c].append(jnp.sum(out_col * state, axis=0, keepdims=True))
            states = tuple(updated)
        if with_read:
            for c in range(chunks):
                result_ref[pl.ds(first, 8), pl.ds(c * LANES, LANES)] = jnp.concatenate(reads[c], 0)
        return states

    states = tuple(init_ref[:, pl.ds(c * LANES, LANES)] for c in range(chunks))
    states = lax.fori_loop(0, length // 8, body, states)
    if not with_read:
        for c in range(chunks):
            result_ref[:, pl.ds(c * LANES, LANES)] = states[c]


def run_scan(step, drive, rate, in_wide, out_wide, init, with_read):
    length, channels = step.shape
    entries = rate.shape[0]
    rows_spec = pl.BlockSpec((length, CHANNEL_BLOCK), lambda j: (0, j))
    state_spec = pl.BlockSpec((entries, CHANNEL_BLOCK), lambda j: (0, j))
    wide_spec = pl.BlockSpec((length, entries, LANES), lambda j: (0, 0, 0))
    shape = (length, channels) if with_read else (entries, channels)
    return pl.pallas_call(
        functools.partial(scan_kernel, with_read=with_read),
        grid=(channels // CHANNEL_BLOCK,),
        in_specs=[rows_spec, rows_spec, state_spec, wide_spec, wide_spec, state_spec],
        out_specs=rows_spec if with_read else state_spec,
        out_shape=jax.ShapeDtypeStruct(shape, jnp.float32),
        interpret=INTERPRET,
    )(step, drive, rate, in_wide, out_wide, init)


def exchange_send(step_sum, local_end, joined):
    count = lax.axis_size("seq")
    entries, channels = local_end.shape
    packed = jnp.concatenate([step_sum[None], local_end], 0).reshape(entries + 1, count, -1)
    packed, joined = lax.optimization_barrier((packed, joined))
    return lax.all_to_all(packed, "seq", 1, 1, tiled=True), joined


def exchange_prefix(gathered, rate):
    count, width = gathered.shape[1:]
    sums = gathered[0]
    ends = jnp.transpose(gathered[1:], (1, 0, 2))
    me = lax.axis_index("seq")
    rate_block = lax.dynamic_slice_in_dim(rate, me * width, width, 1)
    place = jnp.arange(count)
    between = (place[None, :, None] < place[None, None, :]) & (
        place[None, None, :] < place[:, None, None]
    )
    gap = jnp.dot(
        between.reshape(count * count, count).astype(jnp.float32),
        sums,
        precision=lax.Precision.HIGHEST,
    ).reshape(count, count, width)
    before = place[None, :] < place[:, None]
    weight = jnp.where(
        before[:, :, None, None], jnp.exp(rate_block[None, None] * gap[:, :, None, :]), 0.0
    )
    return jnp.sum(weight * ends[None], axis=1)


def exchange_return(incoming):
    count, entries, width = incoming.shape
    back = lax.all_to_all(jnp.transpose(incoming, (1, 0, 2)), "seq", 1, 1, tiled=True)
    return back.reshape(entries, count * width)


def per_device(
    inner_x,
    inner_gate,
    conv_weight,
    conv_bias,
    step_low,
    step_proj,
    step_bias,
    decay_log,
    state_in,
    state_out,
    skip_gain,
    query_heads,
    key_heads,
    value_heads,
):
    reach = conv_weight.shape[0] - 1
    rim = shifted(inner_x[-reach:], "seq", 1)
    rim, query_heads, key_heads, value_heads = lax.optimization_barrier(
        (rim, query_heads, key_heads, value_heads)
    )
    conv = convolve(jnp.concatenate([rim, inner_x], 0), conv_weight, conv_bias)
    step = jax.nn.softplus(
        jnp.dot(step_low, step_proj, preferred_element_type=jnp.float32) + step_bias[None, :]
    )
    rate = -jnp.exp(decay_log)
    drive = step * conv
    length, entries = state_in.shape
    in_wide = jnp.broadcast_to(state_in[:, :, None], (length, entries, LANES))
    out_wide = jnp.broadcast_to(state_out[:, :, None], (length, entries, LANES))
    zero_state = jnp.zeros(rate.shape, jnp.float32)
    local_end = run_scan(step, drive, rate, in_wide, out_wide, zero_state, False)
    tokens = query_heads.shape[0]
    joined = send_heads(
        query_heads.reshape(tokens, -1, HEAD_DIM),
        key_heads.reshape(tokens, -1, HEAD_DIM),
        value_heads.reshape(tokens, -1, HEAD_DIM),
    )
    gathered, joined = exchange_send(jnp.sum(step, axis=0), local_end, joined)
    prefix = []

    def midway(early, heads_first):
        arrived, early = lax.optimization_barrier((gathered, early))
        prefix.append(exchange_prefix(arrived, rate))
        return lax.optimization_barrier((early, prefix[0], heads_first))[::2]

    attention_out = attend_by_heads(joined, tokens, midway)
    incoming = exchange_return(prefix[0])
    read = run_scan(step, drive, rate, in_wide, out_wide, incoming, True)
    mamba_out = (
        (read + skip_gain[None, :] * conv) * jax.nn.silu(inner_gate.astype(jnp.float32))
    ).astype(jnp.bfloat16)
    return (mamba_out, attention_out)


def solution(mesh):
    in_specs = (
        P(("stream", "seq"), None),
        P(("stream", "seq"), None),
        P(),
        P(),
        P(("stream", "seq"), None),
        P(),
        P(),
        P(),
        P(("stream", "seq"), None),
        P(("stream", "seq"), None),
        P(),
        P(("stream", "seq"), None),
        P(("stream", "seq"), None),
        P(("stream", "seq"), None),
    )
    out_specs = (P(("stream", "seq"), None), P(("stream", "seq"), None))
    return jax.shard_map(
        per_device, mesh=mesh, in_specs=in_specs, out_specs=out_specs, check_vma=False
    )
```

```python
import functools
import math

import jax
import jax.numpy as jnp
from jax import lax
from jax.experimental import pallas as pl
from jax.sharding import PartitionSpec as P

HEAD_DIM = 128
LANES = 128
CHANNEL_BLOCK = 512
INTERPRET = False


def shifted(block, axis, distance):
    devices = range(lax.axis_size(axis))
    route = [(i - distance, i) for i in devices if i - distance in devices]
    return lax.ppermute(block, axis, route)


def convolve(padded, conv_weight, conv_bias):
    reach = conv_weight.shape[0] - 1
    length = padded.shape[0] - reach
    total = jnp.zeros((length, padded.shape[1]), jnp.float32)
    for index in range(reach + 1):
        total = total + conv_weight[index][None, :] * padded[index : index + length].astype(
            jnp.float32
        )
    return jax.nn.silu(total + conv_bias[None, :])


def send_heads(q_three, k_three, v_three):
    tokens, heads = q_three.shape[:2]
    count = lax.axis_size("seq")
    group = heads // k_three.shape[1]
    k_wide = jnp.repeat(k_three, group, axis=1)
    v_wide = jnp.repeat(v_three, group, axis=1)
    joined = jnp.concatenate([q_three, k_wide, v_wide], 2).reshape(tokens, count, heads // count, -1)
    arrived = lax.all_to_all(
        jnp.transpose(joined, (1, 0, 2, 3)), "seq", split_axis=0, concat_axis=0, tiled=True
    )
    return arrived.reshape(count * tokens, heads // count, -1)


def attention_kernel(q_ref, k_ref, v_ref, o_ref, *, tile, scale, first):
    index = pl.program_id(1) + first
    query = q_ref[0]
    rows = lax.broadcasted_iota(jnp.int32, (tile, tile), 0)
    cols = lax.broadcasted_iota(jnp.int32, (tile, tile), 1)
    diagonal = rows >= cols

    def scores(j):
        keys = k_ref[0, pl.ds(pl.multiple_of(j * tile, tile), tile), :]
        product = lax.dot_general(
            query, keys, (((1,), (1,)), ((), ())), preferred_element_type=jnp.float32
        )
        return product * scale

    def add_block(j, masked, carry):
        peak, total, summed = carry
        fresh = jnp.maximum(peak, jnp.max(masked, axis=1, keepdims=True))
        shrink = jnp.exp(peak - fresh)
        expo = jnp.exp(masked - fresh)
        values = v_ref[0, pl.ds(pl.multiple_of(j * tile, tile), tile), :]
        summed = shrink * summed + lax.dot_general(
            expo.astype(jnp.bfloat16), values, (((1,), (0,)), ((), ())),
            preferred_element_type=jnp.float32,
        )
        return fresh, shrink * total + jnp.sum(expo, axis=1, keepdims=True), summed

    def sum_step(j, carry):
        return add_block(j, scores(j), carry)

    carry = (
        jnp.full((tile, 1), -1e30, jnp.float32),
        jnp.zeros((tile, 1), jnp.float32),
        jnp.zeros((tile, HEAD_DIM), jnp.float32),
    )
    carry = lax.fori_loop(0, index, sum_step, carry)
    peak, total, summed = add_block(index, jnp.where(diagonal, scores(index), -jnp.inf), carry)
    o_ref[0] = (summed / total).astype(o_ref.dtype)


def attend_heads(q_all, k_all, v_all, first, blocks):
    heads, length, _ = q_all.shape
    tile = length // blocks
    head_spec = pl.BlockSpec((1, length, HEAD_DIM), lambda h, i: (h, 0, 0))
    tile_spec = pl.BlockSpec((1, tile, HEAD_DIM), lambda h, i: (h, i + first, 0))
    out_spec = pl.BlockSpec((1, tile, HEAD_DIM), lambda h, i: (h, i, 0))
    return pl.pallas_call(
        functools.partial(attention_kernel, tile=tile, scale=HEAD_DIM ** (-0.5), first=first),
        grid=(heads, blocks // 2),
        in_specs=[tile_spec, head_spec, head_spec],
        out_specs=out_spec,
        out_shape=jax.ShapeDtypeStruct((heads, length // 2, HEAD_DIM), jnp.bfloat16),
        interpret=INTERPRET,
    )(q_all, k_all, v_all)


def attend_by_heads(joined, tokens, midway):
    length = joined.shape[0]
    blocks = length // math.gcd(length, 512)
    heads_first = [jnp.transpose(x, (1, 0, 2)) for x in (
        joined[:, :, :HEAD_DIM], joined[:, :, HEAD_DIM : 2 * HEAD_DIM], joined[:, :, 2 * HEAD_DIM :]
    )]
    early, heads_first = midway(attend_heads(*heads_first, 0, blocks), heads_first)
    late = attend_heads(*heads_first, blocks // 2, blocks)
    merged = jnp.transpose(jnp.concatenate([early, late], 1), (1, 0, 2))
    length = merged.shape[0]
    count = length // tokens
    back = lax.all_to_all(
        merged.reshape(count, tokens, -1), "seq", split_axis=0, concat_axis=0, tiled=True
    )
    return jnp.transpose(back, (1, 0, 2)).reshape(tokens, -1)


def scan_kernel(step_ref, drive_ref, rate_ref, in_ref, out_ref, init_ref, result_ref, *, with_read):
    length = step_ref.shape[0]
    chunks = step_ref.shape[1] // LANES

    def body(i, states):
        first = pl.multiple_of(i * 8, 8)
        steps = [step_ref[pl.ds(first, 8), pl.ds(c * LANES, LANES)] for c in range(chunks)]
        drives = [drive_ref[pl.ds(first, 8), pl.ds(c * LANES, LANES)] for c in range(chunks)]
        reads = [[] for c in range(chunks)]
        for r in range(8):
            in_col = in_ref[first + r]
            out_col = out_ref[first + r]
            updated = []
            for c in range(chunks):
                decay = jnp.exp(steps[c][r : r + 1] * rate_ref[:, pl.ds(c * LANES, LANES)])
                state = decay * states[c] + drives[c][r : r + 1] * in_col
                updated.append(state)
                if with_read:
                    reads[c].append(jnp.sum(out_col * state, axis=0, keepdims=True))
            states = tuple(updated)
        if with_read:
            for c in range(chunks):
                result_ref[pl.ds(first, 8), pl.ds(c * LANES, LANES)] = jnp.concatenate(reads[c], 0)
        return states

    states = tuple(init_ref[:, pl.ds(c * LANES, LANES)] for c in range(chunks))
    states = lax.fori_loop(0, length // 8, body, states)
    if not with_read:
        for c in range(chunks):
            result_ref[:, pl.ds(c * LANES, LANES)] = states[c]


def run_scan(step, drive, rate, in_wide, out_wide, init, with_read):
    length, channels = step.shape
    entries = rate.shape[0]
    rows_spec = pl.BlockSpec((length, CHANNEL_BLOCK), lambda j: (0, j))
    state_spec = pl.BlockSpec((entries, CHANNEL_BLOCK), lambda j: (0, j))
    wide_spec = pl.BlockSpec((length, entries, LANES), lambda j: (0, 0, 0))
    shape = (length, channels) if with_read else (entries, channels)
    return pl.pallas_call(
        functools.partial(scan_kernel, with_read=with_read),
        grid=(channels // CHANNEL_BLOCK,),
        in_specs=[rows_spec, rows_spec, state_spec, wide_spec, wide_spec, state_spec],
        out_specs=rows_spec if with_read else state_spec,
        out_shape=jax.ShapeDtypeStruct(shape, jnp.float32),
        interpret=INTERPRET,
    )(step, drive, rate, in_wide, out_wide, init)


def exchange_send(step_sum, local_end, joined):
    count = lax.axis_size("seq")
    entries, channels = local_end.shape
    packed = jnp.concatenate([step_sum[None], local_end], 0).reshape(entries + 1, count, -1)
    packed, joined = lax.optimization_barrier((packed, joined))
    return lax.all_to_all(packed, "seq", 1, 1, tiled=True), joined


def exchange_prefix(gathered, rate):
    count, width = gathered.shape[1:]
    sums = gathered[0]
    ends = jnp.transpose(gathered[1:], (1, 0, 2))
    me = lax.axis_index("seq")
    rate_block = lax.dynamic_slice_in_dim(rate, me * width, width, 1)
    place = jnp.arange(count)
    between = (place[None, :, None] < place[None, None, :]) & (
        place[None, None, :] < place[:, None, None]
    )
    gap = jnp.dot(
        between.reshape(count * count, count).astype(jnp.float32),
        sums,
        precision=lax.Precision.HIGHEST,
    ).reshape(count, count, width)
    before = place[None, :] < place[:, None]
    weight = jnp.where(
        before[:, :, None, None], jnp.exp(rate_block[None, None] * gap[:, :, None, :]), 0.0
    )
    return jnp.sum(weight * ends[None], axis=1)


def exchange_return(incoming):
    count, entries, width = incoming.shape
    back = lax.all_to_all(jnp.transpose(incoming, (1, 0, 2)), "seq", 1, 1, tiled=True)
    return back.reshape(entries, count * width)


def per_device(
    inner_x,
    inner_gate,
    conv_weight,
    conv_bias,
    step_low,
    step_proj,
    step_bias,
    decay_log,
    state_in,
    state_out,
    skip_gain,
    query_heads,
    key_heads,
    value_heads,
):
    reach = conv_weight.shape[0] - 1
    rim = shifted(inner_x[-reach:], "seq", 1)
    rim, query_heads, key_heads, value_heads = lax.optimization_barrier(
        (rim, query_heads, key_heads, value_heads)
    )
    conv = convolve(jnp.concatenate([rim, inner_x], 0), conv_weight, conv_bias)
    step = jax.nn.softplus(
        jnp.dot(step_low, step_proj, preferred_element_type=jnp.float32) + step_bias[None, :]
    )
    rate = -jnp.exp(decay_log)
    drive = step * conv
    length, entries = state_in.shape
    in_wide = jnp.broadcast_to(state_in[:, :, None], (length, entries, LANES))
    out_wide = jnp.broadcast_to(state_out[:, :, None], (length, entries, LANES))
    zero_state = jnp.zeros(rate.shape, jnp.float32)
    local_end = run_scan(step, drive, rate, in_wide, out_wide, zero_state, False)
    tokens = query_heads.shape[0]
    joined = send_heads(
        query_heads.reshape(tokens, -1, HEAD_DIM),
        key_heads.reshape(tokens, -1, HEAD_DIM),
        value_heads.reshape(tokens, -1, HEAD_DIM),
    )
    gathered, joined = exchange_send(jnp.sum(step, axis=0), local_end, joined)
    prefix = []

    def midway(early, heads_first):
        arrived, early = lax.optimization_barrier((gathered, early))
        prefix.append(exchange_prefix(arrived, rate))
        return lax.optimization_barrier((early, prefix[0], heads_first))[::2]

    attention_out = attend_by_heads(joined, tokens, midway)
    incoming = exchange_return(prefix[0])
    read = run_scan(step, drive, rate, in_wide, out_wide, incoming, True)
    mamba_out = (
        (read + skip_gain[None, :] * conv) * jax.nn.silu(inner_gate.astype(jnp.float32))
    ).astype(jnp.bfloat16)
    return (mamba_out, attention_out)


def solution(mesh):
    in_specs = (
        P(("stream", "seq"), None),
        P(("stream", "seq"), None),
        P(),
        P(),
        P(("stream", "seq"), None),
        P(),
        P(),
        P(),
        P(("stream", "seq"), None),
        P(("stream", "seq"), None),
        P(),
        P(("stream", "seq"), None),
        P(("stream", "seq"), None),
        P(("stream", "seq"), None),
    )
    out_specs = (P(("stream", "seq"), None), P(("stream", "seq"), None))
    return jax.shard_map(
        per_device, mesh=mesh, in_specs=in_specs, out_specs=out_specs, check_vma=False
    )
```

```python
import functools
import math

import jax
import jax.numpy as jnp
from jax import lax
from jax.experimental import pallas as pl
from jax.sharding import PartitionSpec as P

HEAD_DIM = 128
LANES = 128
CHANNEL_BLOCK = 512
INTERPRET = False


def shifted(block, axis, distance):
    devices = range(lax.axis_size(axis))
    route = [(i - distance, i) for i in devices if i - distance in devices]
    return lax.ppermute(block, axis, route)


def convolve(padded, conv_weight, conv_bias):
    reach = conv_weight.shape[0] - 1
    length = padded.shape[0] - reach
    total = jnp.zeros((length, padded.shape[1]), jnp.float32)
    for index in range(reach + 1):
        total = total + conv_weight[index][None, :] * padded[index : index + length].astype(
            jnp.float32
        )
    return jax.nn.silu(total + conv_bias[None, :])


def pack_kernel(q_ref, k_ref, v_ref, o_ref):
    for i in range(o_ref.shape[1]):
        head = pl.ds(i * HEAD_DIM, HEAD_DIM)
        o_ref[0, i, :, pl.ds(0, HEAD_DIM)] = q_ref[:, head]
        o_ref[0, i, :, pl.ds(HEAD_DIM, HEAD_DIM)] = k_ref[...]
        o_ref[0, i, :, pl.ds(2 * HEAD_DIM, HEAD_DIM)] = v_ref[...]


def send_heads(query_heads, key_heads, value_heads):
    tokens = query_heads.shape[0]
    heads = query_heads.shape[1] // HEAD_DIM
    count = lax.axis_size("seq")
    local = heads // count
    group = heads // (key_heads.shape[1] // HEAD_DIM)
    assert group % local == 0
    kv_spec = pl.BlockSpec((tokens, HEAD_DIM), lambda j: (0, j * local // group))
    joined = pl.pallas_call(
        pack_kernel,
        grid=(count,),
        in_specs=[pl.BlockSpec((tokens, local * HEAD_DIM), lambda j: (0, j)), kv_spec, kv_spec],
        out_specs=pl.BlockSpec((1, local, tokens, 3 * HEAD_DIM), lambda j: (j, 0, 0, 0)),
        out_shape=jax.ShapeDtypeStruct((count, local, tokens, 3 * HEAD_DIM), query_heads.dtype),
        interpret=INTERPRET,
    )(query_heads, key_heads, value_heads)
    arrived = lax.all_to_all(joined, "seq", split_axis=0, concat_axis=0, tiled=True)
    return jnp.transpose(arrived, (1, 0, 2, 3)).reshape(local, count * tokens, -1)


def attention_kernel(q_ref, k_ref, v_ref, o_ref, *, tile, scale, first):
    index = pl.program_id(1) + first
    query = q_ref[0]
    rows = lax.broadcasted_iota(jnp.int32, (tile, tile), 0)
    cols = lax.broadcasted_iota(jnp.int32, (tile, tile), 1)
    diagonal = rows >= cols

    def scores(j):
        keys = k_ref[0, pl.ds(pl.multiple_of(j * tile, tile), tile), :]
        product = lax.dot_general(
            query, keys, (((1,), (1,)), ((), ())), preferred_element_type=jnp.float32
        )
        return product * scale

    def add_block(j, masked, carry):
        peak, total, summed = carry
        fresh = jnp.maximum(peak, jnp.max(masked, axis=1, keepdims=True))
        shrink = jnp.exp(peak - fresh)
        expo = jnp.exp(masked - fresh)
        values = v_ref[0, pl.ds(pl.multiple_of(j * tile, tile), tile), :]
        summed = shrink * summed + lax.dot_general(
            expo.astype(jnp.bfloat16), values, (((1,), (0,)), ((), ())),
            preferred_element_type=jnp.float32,
        )
        return fresh, shrink * total + jnp.sum(expo, axis=1, keepdims=True), summed

    def sum_step(j, carry):
        return add_block(j, scores(j), carry)

    carry = (
        jnp.full((tile, 1), -1e30, jnp.float32),
        jnp.zeros((tile, 1), jnp.float32),
        jnp.zeros((tile, HEAD_DIM), jnp.float32),
    )
    carry = lax.fori_loop(0, index, sum_step, carry)
    peak, total, summed = add_block(index, jnp.where(diagonal, scores(index), -jnp.inf), carry)
    o_ref[0] = (summed / total).astype(o_ref.dtype)


def attend_heads(joined, first, blocks):
    heads, length, _ = joined.shape
    tile = length // blocks
    key_spec = pl.BlockSpec((1, length, HEAD_DIM), lambda h, i: (h, 0, 1))
    value_spec = pl.BlockSpec((1, length, HEAD_DIM), lambda h, i: (h, 0, 2))
    tile_spec = pl.BlockSpec((1, tile, HEAD_DIM), lambda h, i: (h, i + first, 0))
    out_spec = pl.BlockSpec((1, tile, HEAD_DIM), lambda h, i: (h, i, 0))
    return pl.pallas_call(
        functools.partial(attention_kernel, tile=tile, scale=HEAD_DIM ** (-0.5), first=first),
        grid=(heads, blocks // 2),
        in_specs=[tile_spec, key_spec, value_spec],
        out_specs=out_spec,
        out_shape=jax.ShapeDtypeStruct((heads, length // 2, HEAD_DIM), jnp.bfloat16),
        interpret=INTERPRET,
    )(joined, joined, joined)


def attend_by_heads(joined, tokens, midway):
    length = joined.shape[1]
    blocks = length // math.gcd(length, 512)
    early, joined = midway(attend_heads(joined, 0, blocks), joined)
    late = attend_heads(joined, blocks // 2, blocks)
    merged = jnp.transpose(jnp.concatenate([early, late], 1), (1, 0, 2))
    count = length // tokens
    back = lax.all_to_all(
        merged.reshape(count, tokens, -1), "seq", split_axis=0, concat_axis=0, tiled=True
    )
    return jnp.transpose(back, (1, 0, 2)).reshape(tokens, -1)


def scan_kernel(step_ref, drive_ref, rate_ref, in_ref, out_ref, init_ref, result_ref, *, with_read):
    length = step_ref.shape[0]
    chunks = step_ref.shape[1] // LANES

    def body(i, states):
        first = pl.multiple_of(i * 8, 8)
        steps = [step_ref[pl.ds(first, 8), pl.ds(c * LANES, LANES)] for c in range(chunks)]
        drives = [drive_ref[pl.ds(first, 8), pl.ds(c * LANES, LANES)] for c in range(chunks)]
        reads = [[] for c in range(chunks)]
        for r in range(8):
            in_col = in_ref[first + r]
            out_col = out_ref[first + r]
            updated = []
            for c in range(chunks):
                decay = jnp.exp(steps[c][r : r + 1] * rate_ref[:, pl.ds(c * LANES, LANES)])
                state = decay * states[c] + drives[c][r : r + 1] * in_col
                updated.append(state)
                if with_read:
                    reads[c].append(jnp.sum(out_col * state, axis=0, keepdims=True))
            states = tuple(updated)
        if with_read:
            for c in range(chunks):
                result_ref[pl.ds(first, 8), pl.ds(c * LANES, LANES)] = jnp.concatenate(reads[c], 0)
        return states

    states = tuple(init_ref[:, pl.ds(c * LANES, LANES)] for c in range(chunks))
    states = lax.fori_loop(0, length // 8, body, states)
    if not with_read:
        for c in range(chunks):
            result_ref[:, pl.ds(c * LANES, LANES)] = states[c]


def run_scan(step, drive, rate, in_wide, out_wide, init, with_read):
    length, channels = step.shape
    entries = rate.shape[0]
    rows_spec = pl.BlockSpec((length, CHANNEL_BLOCK), lambda j: (0, j))
    state_spec = pl.BlockSpec((entries, CHANNEL_BLOCK), lambda j: (0, j))
    wide_spec = pl.BlockSpec((length, entries, LANES), lambda j: (0, 0, 0))
    shape = (length, channels) if with_read else (entries, channels)
    return pl.pallas_call(
        functools.partial(scan_kernel, with_read=with_read),
        grid=(channels // CHANNEL_BLOCK,),
        in_specs=[rows_spec, rows_spec, state_spec, wide_spec, wide_spec, state_spec],
        out_specs=rows_spec if with_read else state_spec,
        out_shape=jax.ShapeDtypeStruct(shape, jnp.float32),
        interpret=INTERPRET,
    )(step, drive, rate, in_wide, out_wide, init)


def exchange_send(step_sum, local_end, joined):
    count = lax.axis_size("seq")
    entries, channels = local_end.shape
    packed = jnp.concatenate([step_sum[None], local_end], 0).reshape(entries + 1, count, -1)
    packed, joined = lax.optimization_barrier((packed, joined))
    return lax.all_to_all(packed, "seq", 1, 1, tiled=True), joined


def exchange_prefix(gathered, rate):
    count, width = gathered.shape[1:]
    sums = gathered[0]
    ends = jnp.transpose(gathered[1:], (1, 0, 2))
    me = lax.axis_index("seq")
    rate_block = lax.dynamic_slice_in_dim(rate, me * width, width, 1)
    place = jnp.arange(count)
    between = (place[None, :, None] < place[None, None, :]) & (
        place[None, None, :] < place[:, None, None]
    )
    gap = jnp.dot(
        between.reshape(count * count, count).astype(jnp.float32),
        sums,
        precision=lax.Precision.HIGHEST,
    ).reshape(count, count, width)
    before = place[None, :] < place[:, None]
    weight = jnp.where(
        before[:, :, None, None], jnp.exp(rate_block[None, None] * gap[:, :, None, :]), 0.0
    )
    return jnp.sum(weight * ends[None], axis=1)


def exchange_return(incoming):
    count, entries, width = incoming.shape
    back = lax.all_to_all(jnp.transpose(incoming, (1, 0, 2)), "seq", 1, 1, tiled=True)
    return back.reshape(entries, count * width)


def per_device(
    inner_x,
    inner_gate,
    conv_weight,
    conv_bias,
    step_low,
    step_proj,
    step_bias,
    decay_log,
    state_in,
    state_out,
    skip_gain,
    query_heads,
    key_heads,
    value_heads,
):
    reach = conv_weight.shape[0] - 1
    rim = shifted(inner_x[-reach:], "seq", 1)
    rim, query_heads, key_heads, value_heads = lax.optimization_barrier(
        (rim, query_heads, key_heads, value_heads)
    )
    conv = convolve(jnp.concatenate([rim, inner_x], 0), conv_weight, conv_bias)
    step = jax.nn.softplus(
        jnp.dot(step_low, step_proj, preferred_element_type=jnp.float32) + step_bias[None, :]
    )
    rate = -jnp.exp(decay_log)
    drive = step * conv
    length, entries = state_in.shape
    in_wide = jnp.broadcast_to(state_in[:, :, None], (length, entries, LANES))
    out_wide = jnp.broadcast_to(state_out[:, :, None], (length, entries, LANES))
    zero_state = jnp.zeros(rate.shape, jnp.float32)
    local_end = run_scan(step, drive, rate, in_wide, out_wide, zero_state, False)
    tokens = query_heads.shape[0]
    joined = send_heads(query_heads, key_heads, value_heads)
    gathered, joined = exchange_send(jnp.sum(step, axis=0), local_end, joined)
    prefix = []

    def midway(early, heads_first):
        arrived, early = lax.optimization_barrier((gathered, early))
        prefix.append(exchange_prefix(arrived, rate))
        return lax.optimization_barrier((early, prefix[0], heads_first))[::2]

    attention_out = attend_by_heads(joined, tokens, midway)
    incoming = exchange_return(prefix[0])
    read = run_scan(step, drive, rate, in_wide, out_wide, incoming, True)
    mamba_out = (
        (read + skip_gain[None, :] * conv) * jax.nn.silu(inner_gate.astype(jnp.float32))
    ).astype(jnp.bfloat16)
    return (mamba_out, attention_out)


def solution(mesh):
    in_specs = (
        P(("stream", "seq"), None),
        P(("stream", "seq"), None),
        P(),
        P(),
        P(("stream", "seq"), None),
        P(),
        P(),
        P(),
        P(("stream", "seq"), None),
        P(("stream", "seq"), None),
        P(),
        P(("stream", "seq"), None),
        P(("stream", "seq"), None),
        P(("stream", "seq"), None),
    )
    out_specs = (P(("stream", "seq"), None), P(("stream", "seq"), None))
    return jax.shard_map(
        per_device, mesh=mesh, in_specs=in_specs, out_specs=out_specs, check_vma=False
    )
```

```python
import functools
import math

import jax
import jax.numpy as jnp
from jax import lax
from jax.experimental import pallas as pl
from jax.sharding import PartitionSpec as P

HEAD_DIM = 128
LANES = 128
CHANNEL_BLOCK = 512
INTERPRET = False


def shifted(block, axis, distance):
    devices = range(lax.axis_size(axis))
    route = [(i - distance, i) for i in devices if i - distance in devices]
    return lax.ppermute(block, axis, route)


def convolve(padded, conv_weight, conv_bias):
    reach = conv_weight.shape[0] - 1
    length = padded.shape[0] - reach
    total = jnp.zeros((length, padded.shape[1]), jnp.float32)
    for index in range(reach + 1):
        total = total + conv_weight[index][None, :] * padded[index : index + length].astype(
            jnp.float32
        )
    return jax.nn.silu(total + conv_bias[None, :])


def pack_kernel(q_ref, k_ref, v_ref, o_ref, *, group):
    count, local = o_ref.shape[:2]
    for j in range(count):
        for i in range(local):
            head = j * local + i
            kv = pl.ds(head // group * HEAD_DIM, HEAD_DIM)
            o_ref[j, i, :, pl.ds(0, HEAD_DIM)] = q_ref[:, pl.ds(head * HEAD_DIM, HEAD_DIM)]
            o_ref[j, i, :, pl.ds(HEAD_DIM, HEAD_DIM)] = k_ref[:, kv]
            o_ref[j, i, :, pl.ds(2 * HEAD_DIM, HEAD_DIM)] = v_ref[:, kv]


def send_heads(query_heads, key_heads, value_heads):
    tokens = query_heads.shape[0]
    heads = query_heads.shape[1] // HEAD_DIM
    count = lax.axis_size("seq")
    local = heads // count
    group = heads // (key_heads.shape[1] // HEAD_DIM)
    joined = pl.pallas_call(
        functools.partial(pack_kernel, group=group),
        out_shape=jax.ShapeDtypeStruct((count, local, tokens, 3 * HEAD_DIM), query_heads.dtype),
        interpret=INTERPRET,
    )(query_heads, key_heads, value_heads)
    arrived = lax.all_to_all(joined, "seq", split_axis=0, concat_axis=0, tiled=True)
    return jnp.transpose(arrived, (1, 0, 2, 3)).reshape(local, count * tokens, -1)


def attention_kernel(q_ref, k_ref, v_ref, o_ref, *, tile, scale, first):
    index = pl.program_id(1) + first
    query = q_ref[0]
    rows = lax.broadcasted_iota(jnp.int32, (tile, tile), 0)
    cols = lax.broadcasted_iota(jnp.int32, (tile, tile), 1)
    diagonal = rows >= cols

    def scores(j):
        keys = k_ref[0, pl.ds(pl.multiple_of(j * tile, tile), tile), :]
        product = lax.dot_general(
            query, keys, (((1,), (1,)), ((), ())), preferred_element_type=jnp.float32
        )
        return product * scale

    def add_block(j, masked, carry):
        peak, total, summed = carry
        fresh = jnp.maximum(peak, jnp.max(masked, axis=1, keepdims=True))
        shrink = jnp.exp(peak - fresh)
        expo = jnp.exp(masked - fresh)
        values = v_ref[0, pl.ds(pl.multiple_of(j * tile, tile), tile), :]
        summed = shrink * summed + lax.dot_general(
            expo.astype(jnp.bfloat16), values, (((1,), (0,)), ((), ())),
            preferred_element_type=jnp.float32,
        )
        return fresh, shrink * total + jnp.sum(expo, axis=1, keepdims=True), summed

    def sum_step(j, carry):
        return add_block(j, scores(j), carry)

    carry = (
        jnp.full((tile, 1), -1e30, jnp.float32),
        jnp.zeros((tile, 1), jnp.float32),
        jnp.zeros((tile, HEAD_DIM), jnp.float32),
    )
    carry = lax.fori_loop(0, index, sum_step, carry)
    peak, total, summed = add_block(index, jnp.where(diagonal, scores(index), -jnp.inf), carry)
    o_ref[0] = (summed / total).astype(o_ref.dtype)


def attend_heads(joined, first, blocks):
    heads, length, _ = joined.shape
    tile = length // blocks
    key_spec = pl.BlockSpec((1, length, HEAD_DIM), lambda h, i: (h, 0, 1))
    value_spec = pl.BlockSpec((1, length, HEAD_DIM), lambda h, i: (h, 0, 2))
    tile_spec = pl.BlockSpec((1, tile, HEAD_DIM), lambda h, i: (h, i + first, 0))
    out_spec = pl.BlockSpec((1, tile, HEAD_DIM), lambda h, i: (h, i, 0))
    return pl.pallas_call(
        functools.partial(attention_kernel, tile=tile, scale=HEAD_DIM ** (-0.5), first=first),
        grid=(heads, blocks // 2),
        in_specs=[tile_spec, key_spec, value_spec],
        out_specs=out_spec,
        out_shape=jax.ShapeDtypeStruct((heads, length // 2, HEAD_DIM), jnp.bfloat16),
        interpret=INTERPRET,
    )(joined, joined, joined)


def attend_by_heads(joined, tokens, midway):
    length = joined.shape[1]
    blocks = length // math.gcd(length, 512)
    early, joined = midway(attend_heads(joined, 0, blocks), joined)
    late = attend_heads(joined, blocks // 2, blocks)
    merged = jnp.transpose(jnp.concatenate([early, late], 1), (1, 0, 2))
    count = length // tokens
    back = lax.all_to_all(
        merged.reshape(count, tokens, -1), "seq", split_axis=0, concat_axis=0, tiled=True
    )
    return jnp.transpose(back, (1, 0, 2)).reshape(tokens, -1)


def scan_kernel(step_ref, drive_ref, rate_ref, in_ref, out_ref, init_ref, result_ref, *, with_read):
    length = step_ref.shape[0]
    chunks = step_ref.shape[1] // LANES

    def body(i, states):
        first = pl.multiple_of(i * 8, 8)
        steps = [step_ref[pl.ds(first, 8), pl.ds(c * LANES, LANES)] for c in range(chunks)]
        drives = [drive_ref[pl.ds(first, 8), pl.ds(c * LANES, LANES)] for c in range(chunks)]
        reads = [[] for c in range(chunks)]
        for r in range(8):
            in_col = in_ref[first + r]
            out_col = out_ref[first + r]
            updated = []
            for c in range(chunks):
                decay = jnp.exp(steps[c][r : r + 1] * rate_ref[:, pl.ds(c * LANES, LANES)])
                state = decay * states[c] + drives[c][r : r + 1] * in_col
                updated.append(state)
                if with_read:
                    reads[c].append(jnp.sum(out_col * state, axis=0, keepdims=True))
            states = tuple(updated)
        if with_read:
            for c in range(chunks):
                result_ref[pl.ds(first, 8), pl.ds(c * LANES, LANES)] = jnp.concatenate(reads[c], 0)
        return states

    states = tuple(init_ref[:, pl.ds(c * LANES, LANES)] for c in range(chunks))
    states = lax.fori_loop(0, length // 8, body, states)
    if not with_read:
        for c in range(chunks):
            result_ref[:, pl.ds(c * LANES, LANES)] = states[c]


def run_scan(step, drive, rate, in_wide, out_wide, init, with_read):
    length, channels = step.shape
    entries = rate.shape[0]
    rows_spec = pl.BlockSpec((length, CHANNEL_BLOCK), lambda j: (0, j))
    state_spec = pl.BlockSpec((entries, CHANNEL_BLOCK), lambda j: (0, j))
    wide_spec = pl.BlockSpec((length, entries, LANES), lambda j: (0, 0, 0))
    shape = (length, channels) if with_read else (entries, channels)
    return pl.pallas_call(
        functools.partial(scan_kernel, with_read=with_read),
        grid=(channels // CHANNEL_BLOCK,),
        in_specs=[rows_spec, rows_spec, state_spec, wide_spec, wide_spec, state_spec],
        out_specs=rows_spec if with_read else state_spec,
        out_shape=jax.ShapeDtypeStruct(shape, jnp.float32),
        interpret=INTERPRET,
    )(step, drive, rate, in_wide, out_wide, init)


def exchange_send(step_sum, local_end, joined):
    count = lax.axis_size("seq")
    entries, channels = local_end.shape
    packed = jnp.concatenate([step_sum[None], local_end], 0).reshape(entries + 1, count, -1)
    packed, joined = lax.optimization_barrier((packed, joined))
    return lax.all_to_all(packed, "seq", 1, 1, tiled=True), joined


def exchange_prefix(gathered, rate):
    count, width = gathered.shape[1:]
    sums = gathered[0]
    ends = jnp.transpose(gathered[1:], (1, 0, 2))
    me = lax.axis_index("seq")
    rate_block = lax.dynamic_slice_in_dim(rate, me * width, width, 1)
    place = jnp.arange(count)
    between = (place[None, :, None] < place[None, None, :]) & (
        place[None, None, :] < place[:, None, None]
    )
    gap = jnp.dot(
        between.reshape(count * count, count).astype(jnp.float32),
        sums,
        precision=lax.Precision.HIGHEST,
    ).reshape(count, count, width)
    before = place[None, :] < place[:, None]
    weight = jnp.where(
        before[:, :, None, None], jnp.exp(rate_block[None, None] * gap[:, :, None, :]), 0.0
    )
    return jnp.sum(weight * ends[None], axis=1)


def exchange_return(incoming):
    count, entries, width = incoming.shape
    back = lax.all_to_all(jnp.transpose(incoming, (1, 0, 2)), "seq", 1, 1, tiled=True)
    return back.reshape(entries, count * width)


def per_device(
    inner_x,
    inner_gate,
    conv_weight,
    conv_bias,
    step_low,
    step_proj,
    step_bias,
    decay_log,
    state_in,
    state_out,
    skip_gain,
    query_heads,
    key_heads,
    value_heads,
):
    reach = conv_weight.shape[0] - 1
    rim = shifted(inner_x[-reach:], "seq", 1)
    rim, query_heads, key_heads, value_heads = lax.optimization_barrier(
        (rim, query_heads, key_heads, value_heads)
    )
    conv = convolve(jnp.concatenate([rim, inner_x], 0), conv_weight, conv_bias)
    step = jax.nn.softplus(
        jnp.dot(step_low, step_proj, preferred_element_type=jnp.float32) + step_bias[None, :]
    )
    rate = -jnp.exp(decay_log)
    drive = step * conv
    length, entries = state_in.shape
    in_wide = jnp.broadcast_to(state_in[:, :, None], (length, entries, LANES))
    out_wide = jnp.broadcast_to(state_out[:, :, None], (length, entries, LANES))
    zero_state = jnp.zeros(rate.shape, jnp.float32)
    local_end = run_scan(step, drive, rate, in_wide, out_wide, zero_state, False)
    tokens = query_heads.shape[0]
    joined = send_heads(query_heads, key_heads, value_heads)
    gathered, joined = exchange_send(jnp.sum(step, axis=0), local_end, joined)
    prefix = []

    def midway(early, heads_first):
        arrived, early = lax.optimization_barrier((gathered, early))
        prefix.append(exchange_prefix(arrived, rate))
        return lax.optimization_barrier((early, prefix[0], heads_first))[::2]

    attention_out = attend_by_heads(joined, tokens, midway)
    incoming = exchange_return(prefix[0])
    read = run_scan(step, drive, rate, in_wide, out_wide, incoming, True)
    mamba_out = (
        (read + skip_gain[None, :] * conv) * jax.nn.silu(inner_gate.astype(jnp.float32))
    ).astype(jnp.bfloat16)
    return (mamba_out, attention_out)


def solution(mesh):
    in_specs = (
        P(("stream", "seq"), None),
        P(("stream", "seq"), None),
        P(),
        P(),
        P(("stream", "seq"), None),
        P(),
        P(),
        P(),
        P(("stream", "seq"), None),
        P(("stream", "seq"), None),
        P(),
        P(("stream", "seq"), None),
        P(("stream", "seq"), None),
        P(("stream", "seq"), None),
    )
    out_specs = (P(("stream", "seq"), None), P(("stream", "seq"), None))
    return jax.shard_map(
        per_device, mesh=mesh, in_specs=in_specs, out_specs=out_specs, check_vma=False
    )
```

```python
import functools
import math

import jax
import jax.numpy as jnp
from jax import lax
from jax.experimental import pallas as pl
from jax.sharding import PartitionSpec as P

HEAD_DIM = 128
LANES = 128
CHANNEL_BLOCK = 512
INTERPRET = False


def shifted(block, axis, distance):
    devices = range(lax.axis_size(axis))
    route = [(i - distance, i) for i in devices if i - distance in devices]
    return lax.ppermute(block, axis, route)


def convolve(padded, conv_weight, conv_bias):
    reach = conv_weight.shape[0] - 1
    length = padded.shape[0] - reach
    total = jnp.zeros((length, padded.shape[1]), jnp.float32)
    for index in range(reach + 1):
        total = total + conv_weight[index][None, :] * padded[index : index + length].astype(
            jnp.float32
        )
    return jax.nn.silu(total + conv_bias[None, :])


def pack_kernel(q_ref, k_ref, v_ref, o_ref, *, group):
    count, local = o_ref.shape[:2]
    for j in range(count):
        for i in range(local):
            head = j * local + i
            kv = pl.ds(head // group * HEAD_DIM, HEAD_DIM)
            o_ref[j, i, :, pl.ds(0, HEAD_DIM)] = q_ref[:, pl.ds(head * HEAD_DIM, HEAD_DIM)]
            o_ref[j, i, :, pl.ds(HEAD_DIM, HEAD_DIM)] = k_ref[:, kv]
            o_ref[j, i, :, pl.ds(2 * HEAD_DIM, HEAD_DIM)] = v_ref[:, kv]


def send_heads(query_heads, key_heads, value_heads):
    tokens = query_heads.shape[0]
    heads = query_heads.shape[1] // HEAD_DIM
    count = lax.axis_size("seq")
    local = heads // count
    group = heads // (key_heads.shape[1] // HEAD_DIM)
    joined = pl.pallas_call(
        functools.partial(pack_kernel, group=group),
        out_shape=jax.ShapeDtypeStruct((count, local, tokens, 3 * HEAD_DIM), query_heads.dtype),
        interpret=INTERPRET,
    )(query_heads, key_heads, value_heads)
    arrived = lax.all_to_all(joined, "seq", split_axis=0, concat_axis=0, tiled=True)
    return jnp.transpose(arrived, (1, 0, 2, 3)).reshape(local, count * tokens, -1)


def attention_kernel(q_ref, k_ref, v_ref, o_ref, *, tile, scale, first):
    index = pl.program_id(1) + first
    query = q_ref[0]
    rows = lax.broadcasted_iota(jnp.int32, (tile, tile), 0)
    cols = lax.broadcasted_iota(jnp.int32, (tile, tile), 1)
    diagonal = rows >= cols

    def scores(j):
        keys = k_ref[0, pl.ds(pl.multiple_of(j * tile, tile), tile), :]
        product = lax.dot_general(
            query, keys, (((1,), (1,)), ((), ())), preferred_element_type=jnp.float32
        )
        return product * scale

    def add_block(j, masked, carry):
        peak, total, summed = carry
        fresh = jnp.maximum(peak, jnp.max(masked, axis=1, keepdims=True))
        shrink = jnp.exp(peak - fresh)
        expo = jnp.exp(masked - fresh)
        values = v_ref[0, pl.ds(pl.multiple_of(j * tile, tile), tile), :]
        summed = shrink * summed + lax.dot_general(
            expo.astype(jnp.bfloat16), values, (((1,), (0,)), ((), ())),
            preferred_element_type=jnp.float32,
        )
        return fresh, shrink * total + jnp.sum(expo, axis=1, keepdims=True), summed

    def sum_step(j, carry):
        return add_block(j, scores(j), carry)

    carry = (
        jnp.full((tile, 1), -1e30, jnp.float32),
        jnp.zeros((tile, 1), jnp.float32),
        jnp.zeros((tile, HEAD_DIM), jnp.float32),
    )
    carry = lax.fori_loop(0, index, sum_step, carry)
    peak, total, summed = add_block(index, jnp.where(diagonal, scores(index), -jnp.inf), carry)
    o_ref[0] = (summed / total).astype(o_ref.dtype)


def attend_heads(joined, first, blocks):
    heads, length, _ = joined.shape
    tile = length // blocks
    key_spec = pl.BlockSpec((1, length, HEAD_DIM), lambda h, i: (h, 0, 1))
    value_spec = pl.BlockSpec((1, length, HEAD_DIM), lambda h, i: (h, 0, 2))
    tile_spec = pl.BlockSpec((1, tile, HEAD_DIM), lambda h, i: (h, i + first, 0))
    out_spec = pl.BlockSpec((1, tile, HEAD_DIM), lambda h, i: (h, i, 0))
    return pl.pallas_call(
        functools.partial(attention_kernel, tile=tile, scale=HEAD_DIM ** (-0.5), first=first),
        grid=(heads, blocks // 2),
        in_specs=[tile_spec, key_spec, value_spec],
        out_specs=out_spec,
        out_shape=jax.ShapeDtypeStruct((heads, length // 2, HEAD_DIM), jnp.bfloat16),
        interpret=INTERPRET,
    )(joined, joined, joined)


def attend_by_heads(joined, tokens, midway):
    length = joined.shape[1]
    blocks = length // math.gcd(length, 1024)
    early, joined = midway(attend_heads(joined, 0, blocks), joined)
    late = attend_heads(joined, blocks // 2, blocks)
    merged = jnp.transpose(jnp.concatenate([early, late], 1), (1, 0, 2))
    count = length // tokens
    back = lax.all_to_all(
        merged.reshape(count, tokens, -1), "seq", split_axis=0, concat_axis=0, tiled=True
    )
    return jnp.transpose(back, (1, 0, 2)).reshape(tokens, -1)


def scan_kernel(step_ref, drive_ref, rate_ref, in_ref, out_ref, init_ref, result_ref, *, with_read):
    length = step_ref.shape[0]
    chunks = step_ref.shape[1] // LANES

    def body(i, states):
        first = pl.multiple_of(i * 8, 8)
        steps = [step_ref[pl.ds(first, 8), pl.ds(c * LANES, LANES)] for c in range(chunks)]
        drives = [drive_ref[pl.ds(first, 8), pl.ds(c * LANES, LANES)] for c in range(chunks)]
        reads = [[] for c in range(chunks)]
        for r in range(8):
            in_col = in_ref[first + r]
            out_col = out_ref[first + r]
            updated = []
            for c in range(chunks):
                decay = jnp.exp(steps[c][r : r + 1] * rate_ref[:, pl.ds(c * LANES, LANES)])
                state = decay * states[c] + drives[c][r : r + 1] * in_col
                updated.append(state)
                if with_read:
                    reads[c].append(jnp.sum(out_col * state, axis=0, keepdims=True))
            states = tuple(updated)
        if with_read:
            for c in range(chunks):
                result_ref[pl.ds(first, 8), pl.ds(c * LANES, LANES)] = jnp.concatenate(reads[c], 0)
        return states

    states = tuple(init_ref[:, pl.ds(c * LANES, LANES)] for c in range(chunks))
    states = lax.fori_loop(0, length // 8, body, states)
    if not with_read:
        for c in range(chunks):
            result_ref[:, pl.ds(c * LANES, LANES)] = states[c]


def run_scan(step, drive, rate, in_wide, out_wide, init, with_read):
    length, channels = step.shape
    entries = rate.shape[0]
    rows_spec = pl.BlockSpec((length, CHANNEL_BLOCK), lambda j: (0, j))
    state_spec = pl.BlockSpec((entries, CHANNEL_BLOCK), lambda j: (0, j))
    wide_spec = pl.BlockSpec((length, entries, LANES), lambda j: (0, 0, 0))
    shape = (length, channels) if with_read else (entries, channels)
    return pl.pallas_call(
        functools.partial(scan_kernel, with_read=with_read),
        grid=(channels // CHANNEL_BLOCK,),
        in_specs=[rows_spec, rows_spec, state_spec, wide_spec, wide_spec, state_spec],
        out_specs=rows_spec if with_read else state_spec,
        out_shape=jax.ShapeDtypeStruct(shape, jnp.float32),
        interpret=INTERPRET,
    )(step, drive, rate, in_wide, out_wide, init)


def exchange_send(step_sum, local_end, joined):
    count = lax.axis_size("seq")
    entries, channels = local_end.shape
    packed = jnp.concatenate([step_sum[None], local_end], 0).reshape(entries + 1, count, -1)
    packed, joined = lax.optimization_barrier((packed, joined))
    return lax.all_to_all(packed, "seq", 1, 1, tiled=True), joined


def exchange_prefix(gathered, rate):
    count, width = gathered.shape[1:]
    sums = gathered[0]
    ends = jnp.transpose(gathered[1:], (1, 0, 2))
    me = lax.axis_index("seq")
    rate_block = lax.dynamic_slice_in_dim(rate, me * width, width, 1)
    place = jnp.arange(count)
    between = (place[None, :, None] < place[None, None, :]) & (
        place[None, None, :] < place[:, None, None]
    )
    gap = jnp.dot(
        between.reshape(count * count, count).astype(jnp.float32),
        sums,
        precision=lax.Precision.HIGHEST,
    ).reshape(count, count, width)
    before = place[None, :] < place[:, None]
    weight = jnp.where(
        before[:, :, None, None], jnp.exp(rate_block[None, None] * gap[:, :, None, :]), 0.0
    )
    return jnp.sum(weight * ends[None], axis=1)


def exchange_return(incoming):
    count, entries, width = incoming.shape
    back = lax.all_to_all(jnp.transpose(incoming, (1, 0, 2)), "seq", 1, 1, tiled=True)
    return back.reshape(entries, count * width)


def per_device(
    inner_x,
    inner_gate,
    conv_weight,
    conv_bias,
    step_low,
    step_proj,
    step_bias,
    decay_log,
    state_in,
    state_out,
    skip_gain,
    query_heads,
    key_heads,
    value_heads,
):
    reach = conv_weight.shape[0] - 1
    rim = shifted(inner_x[-reach:], "seq", 1)
    rim, query_heads, key_heads, value_heads = lax.optimization_barrier(
        (rim, query_heads, key_heads, value_heads)
    )
    conv = convolve(jnp.concatenate([rim, inner_x], 0), conv_weight, conv_bias)
    step = jax.nn.softplus(
        jnp.dot(step_low, step_proj, preferred_element_type=jnp.float32) + step_bias[None, :]
    )
    rate = -jnp.exp(decay_log)
    drive = step * conv
    length, entries = state_in.shape
    in_wide = jnp.broadcast_to(state_in[:, :, None], (length, entries, LANES))
    out_wide = jnp.broadcast_to(state_out[:, :, None], (length, entries, LANES))
    zero_state = jnp.zeros(rate.shape, jnp.float32)
    local_end = run_scan(step, drive, rate, in_wide, out_wide, zero_state, False)
    tokens = query_heads.shape[0]
    joined = send_heads(query_heads, key_heads, value_heads)
    gathered, joined = exchange_send(jnp.sum(step, axis=0), local_end, joined)
    prefix = []

    def midway(early, heads_first):
        arrived, early = lax.optimization_barrier((gathered, early))
        prefix.append(exchange_prefix(arrived, rate))
        return lax.optimization_barrier((early, prefix[0], heads_first))[::2]

    attention_out = attend_by_heads(joined, tokens, midway)
    incoming = exchange_return(prefix[0])
    read = run_scan(step, drive, rate, in_wide, out_wide, incoming, True)
    mamba_out = (
        (read + skip_gain[None, :] * conv) * jax.nn.silu(inner_gate.astype(jnp.float32))
    ).astype(jnp.bfloat16)
    return (mamba_out, attention_out)


def solution(mesh):
    in_specs = (
        P(("stream", "seq"), None),
        P(("stream", "seq"), None),
        P(),
        P(),
        P(("stream", "seq"), None),
        P(),
        P(),
        P(),
        P(("stream", "seq"), None),
        P(("stream", "seq"), None),
        P(),
        P(("stream", "seq"), None),
        P(("stream", "seq"), None),
        P(("stream", "seq"), None),
    )
    out_specs = (P(("stream", "seq"), None), P(("stream", "seq"), None))
    return jax.shard_map(
        per_device, mesh=mesh, in_specs=in_specs, out_specs=out_specs, check_vma=False
    )
```
